1024 devices in a mesh: seq: 128 (over z, x, core), head: 8 (over y).
Axes of the slice: x: 4, y: 8, z: 16, core: 2. Of those that a mesh axis runs over, the one named last changes fastest.
Arguments:
- queries: bfloat16 [65536, 2048], P(('seq', 'head')), may hold values from -6 to 6
- key_vectors: bfloat16 [65536, 2048], P(('seq', 'head')), may hold values from -6 to 6
- value_vectors: bfloat16 [65536, 2048], P(('seq', 'head')), may hold values from -6 to 6
- grad_output: bfloat16 [65536, 2048], P(('seq', 'head')), may hold values from -6 to 6
- level_weights: int32 [9, 16, 65536], P(None, 'head', 'seq'), may hold values from 0 to 127
Outputs:
- output: bfloat16 [65536, 2048], P('seq', 'head')
- grad_query: bfloat16 [65536, 2048], P('seq', 'head')
- grad_key: bfloat16 [65536, 2048], P('seq', 'head')
- grad_value: bfloat16 [65536, 2048], P('seq', 'head')
The draws below stay inside these ranges and needn't reach their ends.
All inputs are finite; a program needn't handle non-finite values.
Results may differ from the reference program's by a relative error of at most 0.0057.
Values may be sent and summed in bfloat16 or wider, within the bound.
No kernel may reach another device: no remote copies, remote signals or barrier semaphores. Data moves between devices by JAX's collectives and lax.ppermute only.
A program may use at most 32 MiB of HBM per device.

```python
import jax
import jax.numpy as jnp
from jax import lax

HEADS = 16
D_HEAD = 128
HIDDEN_SIZE = 2048
SPAN = 256
TOKENS = 65536
SPANS = 256
LEVELS = 9


def place_ends(values, own_key, least, high):
    longest = values.shape.index(max(values.shape))
    spots = []
    for shift in (0, 1):
        where = [jax.random.randint(jax.random.fold_in(own_key, axis), (), 0, length) for axis, length in enumerate(values.shape)]
        where[longest] = (where[longest] + shift) % values.shape[longest]
        spots.append(tuple(where))
    return values.at[spots[0]].set(least).at[spots[1]].set(high)


def steps_of(own_key, dims, shards, least, top_value):
    def one(axis_at, blocks):
        steps = jax.random.uniform(jax.random.fold_in(jax.random.fold_in(own_key, 6), axis_at), (blocks,), jnp.float32, least / len(shards), top_value / len(shards))
        return jnp.repeat(jnp.exp(steps), dims[axis_at] // blocks).reshape((-1,) + (1,) * (len(dims) - axis_at - 1))

    level = one(*shards[0])
    for cut in shards[1:]:
        level = level * one(*cut)
    return level


def scatter_about(stream_key, extent, spread, reach, cuts=(), held_as=jnp.bfloat16):
    entries = spread * jax.random.normal(stream_key, extent, jnp.float32)
    if cuts:
        entries = entries * steps_of(stream_key, extent, cuts, -0.22, 0.18)
    return jnp.clip(entries, -reach, reach).astype(held_as)


def setup_inputs(seed: int = 0) -> dict:
    splits = jax.random.split(jax.random.key(seed), 6)
    return {
        "queries": scatter_about(splits[0], (TOKENS, HIDDEN_SIZE), 1.0, 6.0, ((0, 1024),)),
        "key_vectors": scatter_about(splits[1], (TOKENS, HIDDEN_SIZE), 1.0, 6.0, ((0, 1024),)),
        "value_vectors": scatter_about(splits[2], (TOKENS, HIDDEN_SIZE), 1.0, 6.0, ((0, 1024),)),
        "grad_output": scatter_about(splits[3], (TOKENS, HIDDEN_SIZE), 1.0, 6.0, ((0, 1024),)),
        "level_weights": place_ends(jax.random.randint(splits[4], (LEVELS, HEADS, TOKENS), 0, 128), jax.random.fold_in(splits[4], 1), 0, 127).astype(jnp.int32),
    }


def rounded(matrix):
    return lax.optimization_barrier(matrix.astype(jnp.bfloat16)).astype(jnp.float32)


def level_gains():
    values = [(D_HEAD * SPAN) ** -0.5] + [(D_HEAD * 2 ** tree_level * SPAN) ** -0.5 for tree_level in range(LEVELS - 1)]
    return jnp.array(values, dtype=jnp.float32)


def one_head(operands):
    query_rows, key_rows, value_rows, cotan_rows, weight_ints = operands
    query_f = query_rows.astype(jnp.float32)
    key_f = key_rows.astype(jnp.float32)
    value_f = value_rows.astype(jnp.float32)
    cotan_f = cotan_rows.astype(jnp.float32)
    weights = weight_ints.astype(jnp.float32) / 64.0 * level_gains()[:, None, None]
    position = jnp.arange(SPAN, dtype=jnp.int32)
    causal = position[:, None] >= position[None, :]
    scores = jnp.einsum("ctp,cup->ctu", query_f, key_f)
    attention = rounded(jnp.where(causal, scores * weights[0][:, :, None], 0.0))
    cotan_scores = jnp.einsum("ctr,cur->ctu", cotan_f, value_f)
    grad_scores = rounded(jnp.where(causal, cotan_scores * weights[0][:, :, None], 0.0))
    output = jnp.einsum("ctu,cur->ctr", attention, value_f)
    grad_query = jnp.einsum("ctu,cup->ctp", grad_scores, key_f)
    grad_key = jnp.einsum("ctu,ctp->cup", grad_scores, query_f)
    grad_value = jnp.einsum("ctu,ctr->cur", attention, cotan_f)
    states = jnp.einsum("cup,cur->cpr", key_f, value_f)
    span_ids = jnp.arange(SPANS, dtype=jnp.int32)
    grad_states = jnp.zeros((SPANS, D_HEAD, D_HEAD), jnp.float32)
    for tree_level in range(LEVELS - 1):
        groups = SPANS // 2 ** tree_level
        shifted = jnp.right_shift(span_ids, tree_level)
        upper_bit = (shifted % 2).astype(jnp.float32)
        lower_bit = 1.0 - upper_bit
        blocks = states.reshape(groups, 2 ** tree_level, D_HEAD, D_HEAD).sum(axis=1)
        bucket = rounded(blocks[jnp.maximum(shifted - 1, 0)] * upper_bit[:, None, None])
        level_w = weights[tree_level + 1][:, :, None]
        output = output + level_w * jnp.einsum("ctp,cpr->ctr", query_f, bucket)
        grad_query = grad_query + level_w * jnp.einsum("cpr,ctr->ctp", bucket, cotan_f)
        weighted = rounded(level_w * cotan_f)
        state_grad = jnp.einsum("ctp,ctr->cpr", query_f, weighted) * upper_bit[:, None, None]
        grad_blocks = state_grad.reshape(groups, 2 ** tree_level, D_HEAD, D_HEAD).sum(axis=1)
        grad_states = grad_states + grad_blocks[jnp.minimum(shifted + 1, groups - 1)] * lower_bit[:, None, None]
    grad_half = rounded(grad_states)
    grad_key = grad_key + jnp.einsum("cur,cpr->cup", value_f, grad_half)
    grad_value = grad_value + jnp.einsum("cup,cpr->cur", key_f, grad_half)
    return output, grad_query, grad_key, grad_value


def heads_first(matrix):
    return matrix.reshape(SPANS, SPAN, HEADS, D_HEAD).transpose(2, 0, 1, 3)


def restore_layout(stacked):
    return stacked.transpose(1, 2, 0, 3).reshape(TOKENS, HIDDEN_SIZE).astype(jnp.bfloat16)


def reference(queries, key_vectors, value_vectors, grad_output, level_weights):
    weight_heads = level_weights.reshape(LEVELS, HEADS, SPANS, SPAN).transpose(1, 0, 2, 3)
    results = lax.map(one_head, (heads_first(queries), heads_first(key_vectors), heads_first(value_vectors), heads_first(grad_output), weight_heads))
    return (restore_layout(results[0]), restore_layout(results[1]), restore_layout(results[2]), restore_layout(results[3]))
```

```python
import jax
import jax.numpy as jnp
import numpy as np
from jax import lax
from jax.sharding import PartitionSpec as P

SPAN = 256


def swapped(value, axis, distance):
    mask = 2**distance
    pairs = [(source, source ^ mask) for source in range(lax.axis_size(axis))]
    return lax.ppermute(value, axis, pairs)


def bucket_table(per_dev, local_levels):
    level_table = np.zeros((local_levels, per_dev, per_dev), np.float32)
    for target in range(per_dev):
        begin_at = target >> 1 << 1
        end_at = target >> 0 << 0
        level_table[0, target, begin_at:end_at] = 1.0
    return jnp.asarray(level_table)


def body(queries, key_vectors, value_vectors, grad_output, level_weights):
    stacked = jnp.stack([queries, key_vectors, value_vectors, grad_output], axis=1)
    exchanged = lax.all_to_all(stacked, "head", split_axis=2, concat_axis=0, tiled=True)
    query_in, key_in, value_in, cotan_in = (exchanged[:, index] for index in range(4))
    tokens_dev = query_in.shape[0]
    heads_local = level_weights.shape[1]
    head_size = query_in.shape[1] // heads_local
    levels_all = level_weights.shape[0]
    per_dev = tokens_dev // SPAN
    local_levels = per_dev.bit_length() - 1
    cross_levels = lax.axis_size("seq").bit_length() - 1

    def split_spans(matrix):
        return matrix.reshape(per_dev, SPAN, heads_local, head_size)

    query_rows = split_spans(query_in)
    key_rows = split_spans(key_in)
    value_rows = split_spans(value_in)
    cotan_rows = split_spans(cotan_in)
    gain_list = [(head_size * SPAN) ** (-0.5)] + [
        (head_size * 2**tree_level * SPAN) ** (-0.5) for tree_level in range(levels_all - 1)
    ]
    level_gains = jnp.array(gain_list, jnp.float32)
    weights = (level_weights.astype(jnp.float32) / 64.0 * level_gains[:, None, None]).reshape(
        levels_all, heads_local, per_dev, SPAN
    )
    intra_w = jnp.transpose(weights[0], (1, 0, 2))[:, :, :, None]
    inter_w = jnp.transpose(weights[1:], (2, 0, 3, 1))[..., None]
    position = jnp.arange(SPAN, dtype=jnp.int32)
    causal = position[:, None] >= position[None, :]
    scores = jnp.einsum("bthp,buhp->bhtu", query_rows, key_rows, preferred_element_type=jnp.float32)
    attention = jnp.where(causal, scores * intra_w, 0.0).astype(jnp.bfloat16)
    cotan_scores = jnp.einsum(
        "bthr,buhr->bhtu", cotan_rows, value_rows, preferred_element_type=jnp.float32
    )
    grad_scores = jnp.where(causal, cotan_scores * intra_w, 0.0).astype(jnp.bfloat16)
    output = jnp.einsum(
        "bhtu,buhr->bthr", attention, value_rows, preferred_element_type=jnp.float32
    )
    grad_query = jnp.einsum(
        "bhtu,buhp->bthp", grad_scores, key_rows, preferred_element_type=jnp.float32
    )
    grad_key = jnp.einsum(
        "bhtu,bthp->buhp", grad_scores, query_rows, preferred_element_type=jnp.float32
    )
    grad_value = jnp.einsum(
        "bhtu,bthr->buhr", attention, cotan_rows, preferred_element_type=jnp.float32
    )
    states = jnp.einsum("buhp,buhr->bhpr", key_rows, value_rows, preferred_element_type=jnp.float32)
    seq_index = lax.axis_index("seq")
    upper_bits = (jnp.right_shift(seq_index, jnp.arange(cross_levels, dtype=jnp.int32)) % 2).astype(
        jnp.float32
    )
    weighted = (inter_w * cotan_rows[:, None]).astype(jnp.bfloat16)
    level_grads = jnp.einsum(
        "bthp,bmthr->bmhpr", query_rows, weighted, preferred_element_type=jnp.float32
    )
    running = jnp.sum(states, axis=0)
    pending = jnp.sum(level_grads[:, local_levels:], axis=0) * upper_bits[:, None, None, None]
    device_grad = jnp.zeros_like(running)
    cross_list = []
    for tree_bit in range(cross_levels):
        packet = jnp.concatenate([running[None], pending], axis=0)
        arrived = swapped(packet, "seq", tree_bit)
        partner = arrived[0]
        cross_list.append(partner * upper_bits[tree_bit])
        running = running + partner
        device_grad = device_grad + (1.0 - upper_bits[tree_bit]) * arrived[1]
        pending = pending[1:] + arrived[2:]
    level_table = bucket_table(per_dev, local_levels)
    local_buckets = jnp.einsum(
        "mji,ihpr->jmhpr", level_table, states, precision=lax.Precision.HIGHEST
    )
    cross_stack = jnp.stack(cross_list)
    cross_buckets = jnp.broadcast_to(cross_stack[None], (per_dev,) + cross_stack.shape)
    buckets = jnp.concatenate([local_buckets, cross_buckets], axis=1).astype(jnp.bfloat16)
    inter_out = jnp.einsum(
        "bthp,bmhpr->bmthr", query_rows, buckets, preferred_element_type=jnp.float32
    )
    output = output + jnp.sum(inter_w * inter_out, axis=1)
    inter_grad = jnp.einsum(
        "bmhpr,bthr->bmthp", buckets, cotan_rows, preferred_element_type=jnp.float32
    )
    grad_query = grad_query + jnp.sum(inter_w * inter_grad, axis=1)
    local_grad = jnp.einsum(
        "mji,jmhpr->ihpr",
        level_table,
        level_grads[:, :local_levels],
        precision=lax.Precision.HIGHEST,
    )
    state_grad = (local_grad + device_grad[None]).astype(jnp.bfloat16)
    grad_key = grad_key + jnp.einsum(
        "buhr,bhpr->buhp", value_rows, state_grad, preferred_element_type=jnp.float32
    )
    grad_value = grad_value + jnp.einsum(
        "buhp,bhpr->buhr", key_rows, state_grad, preferred_element_type=jnp.float32
    )

    def merge_rows(matrix):
        return matrix.reshape(tokens_dev, heads_local * head_size).astype(jnp.bfloat16)

    return (
        merge_rows(output),
        merge_rows(grad_query),
        merge_rows(grad_key),
        merge_rows(grad_value),
    )


def solution(mesh):
    placed = (
        P(("seq", "head"), None),
        P(("seq", "head"), None),
        P(("seq", "head"), None),
        P(("seq", "head"), None),
        P(None, "head", "seq"),
    )
    return jax.shard_map(
        body,
        mesh=mesh,
        in_specs=placed,
        out_specs=(P("seq", "head"), P("seq", "head"), P("seq", "head"), P("seq", "head")),
        check_vma=False,
    )
```

```python
import jax
import jax.numpy as jnp
import numpy as np
from jax import lax
from jax.sharding import Mesh, PartitionSpec as P

SPAN = 256


def swapped(value, axis, distance):
    mask = 2**distance
    pairs = [(source, source ^ mask) for source in range(lax.axis_size(axis))]
    return lax.ppermute(value, axis, pairs)


def bucket_table(per_dev, local_levels):
    level_table = np.zeros((local_levels, per_dev, per_dev), np.float32)
    for level in range(local_levels):
        for target in range(per_dev):
            begin_at = target >> (level + 1) << (level + 1)
            end_at = target >> level << level
            level_table[level, target, begin_at:end_at] = 1.0
    return jnp.asarray(level_table)


def body(queries, key_vectors, value_vectors, grad_output, level_weights):
    stacked = jnp.stack([queries, key_vectors, value_vectors, grad_output], axis=1)
    exchanged = lax.all_to_all(stacked, "head", split_axis=2, concat_axis=0, tiled=True)
    query_in, key_in, value_in, cotan_in = (exchanged[:, index] for index in range(4))
    tokens_dev = query_in.shape[0]
    heads_local = level_weights.shape[1]
    head_size = query_in.shape[1] // heads_local
    levels_all = level_weights.shape[0]
    per_dev = tokens_dev // SPAN
    local_levels = per_dev.bit_length() - 1
    cross_levels = (lax.axis_size("z") * 8).bit_length() - 1

    def split_spans(matrix):
        return matrix.reshape(per_dev, SPAN, heads_local, head_size)

    query_rows = split_spans(query_in)
    key_rows = split_spans(key_in)
    value_rows = split_spans(value_in)
    cotan_rows = split_spans(cotan_in)
    gain_list = [(head_size * SPAN) ** (-0.5)] + [
        (head_size * 2**tree_level * SPAN) ** (-0.5) for tree_level in range(levels_all - 1)
    ]
    level_gains = jnp.array(gain_list, jnp.float32)
    weights = (level_weights.astype(jnp.float32) / 64.0 * level_gains[:, None, None]).reshape(
        levels_all, heads_local, per_dev, SPAN
    )
    intra_w = jnp.transpose(weights[0], (1, 0, 2))[:, :, :, None]
    inter_w = jnp.transpose(weights[1:], (2, 0, 3, 1))[..., None]
    position = jnp.arange(SPAN, dtype=jnp.int32)
    causal = position[:, None] >= position[None, :]
    scores = jnp.einsum("bthp,buhp->bhtu", query_rows, key_rows, preferred_element_type=jnp.float32)
    attention = jnp.where(causal, scores * intra_w, 0.0).astype(jnp.bfloat16)
    cotan_scores = jnp.einsum(
        "bthr,buhr->bhtu", cotan_rows, value_rows, preferred_element_type=jnp.float32
    )
    grad_scores = jnp.where(causal, cotan_scores * intra_w, 0.0).astype(jnp.bfloat16)
    output = jnp.einsum(
        "bhtu,buhr->bthr", attention, value_rows, preferred_element_type=jnp.float32
    )
    grad_query = jnp.einsum(
        "bhtu,buhp->bthp", grad_scores, key_rows, preferred_element_type=jnp.float32
    )
    grad_key = jnp.einsum(
        "bhtu,bthp->buhp", grad_scores, query_rows, preferred_element_type=jnp.float32
    )
    grad_value = jnp.einsum(
        "bhtu,bthr->buhr", attention, cotan_rows, preferred_element_type=jnp.float32
    )
    states = jnp.einsum("buhp,buhr->bhpr", key_rows, value_rows, preferred_element_type=jnp.float32)
    core_index = lax.axis_index("core")
    x_index = lax.axis_index("x")
    seq_index = (lax.axis_index("z") * 4 + x_index) * 2 + core_index
    upper_bits = (jnp.right_shift(seq_index, jnp.arange(cross_levels, dtype=jnp.int32)) % 2).astype(
        jnp.float32
    )
    weighted = (inter_w * cotan_rows[:, None]).astype(jnp.bfloat16)
    level_grads = jnp.einsum(
        "bthp,bmthr->bmhpr", query_rows, weighted, preferred_element_type=jnp.float32
    )
    running = jnp.sum(states, axis=0)
    pending = jnp.sum(level_grads[:, local_levels:], axis=0) * upper_bits[:, None, None, None]
    packet = jnp.concatenate([running[None], pending], axis=0)
    arrived = swapped(packet, "core", 0)
    cross_first = arrived[0] * upper_bits[0]
    grad_first = (1.0 - upper_bits[0]) * arrived[1]
    running = lax.dynamic_index_in_dim(running + arrived[0], core_index, 0, keepdims=False)
    pending = lax.dynamic_index_in_dim(pending[1:] + arrived[2:], core_index, 1, keepdims=False)
    packet = jnp.concatenate([running[None], pending], axis=0)
    arrived = swapped(packet, "x", 0)
    cross_x1 = arrived[0] * upper_bits[1]
    grad_x1 = (1.0 - upper_bits[1]) * arrived[1]

    def halved(matrix):
        shaped = matrix.reshape(matrix.shape[:-2] + (2, 2, head_size // 4, head_size))
        return lax.dynamic_index_in_dim(shaped, x_index % 2, shaped.ndim - 3, keepdims=False)

    running = halved(running + arrived[0])
    pending = halved(pending[1:] + arrived[2:])
    packet = jnp.concatenate([running[None], pending], axis=0)
    arrived = swapped(packet, "x", 1)
    cross_x2 = arrived[0] * upper_bits[2]
    grad_x2 = (1.0 - upper_bits[2]) * arrived[1]

    def quartered(matrix):
        return lax.dynamic_index_in_dim(matrix, x_index // 2, matrix.ndim - 3, keepdims=False)

    running = quartered(running + arrived[0])
    pending = quartered(pending[1:] + arrived[2:])
    grad_z = jnp.zeros_like(running)
    cross_z = []
    for z_bit in range(cross_levels - 3):
        tree_bit = z_bit + 3
        packet = jnp.concatenate([running[None], pending], axis=0)
        arrived = swapped(packet, "z", z_bit)
        cross_z.append(arrived[0] * upper_bits[tree_bit])
        grad_z = grad_z + (1.0 - upper_bits[tree_bit]) * arrived[1]
        running = running + arrived[0]
        pending = pending[1:] + arrived[2:]

    quarter = head_size // 4
    pieces = jnp.concatenate(
        [
            jnp.stack([cross_x1, grad_x1]).reshape(8, quarter, head_size),
            jnp.stack([cross_x2, grad_x2]).reshape(4, quarter, head_size),
            jnp.stack(cross_z + [grad_z]),
        ]
    )
    gathered = lax.all_gather(pieces, ("x", "core")).reshape((4, 2) + pieces.shape)
    own = lax.dynamic_index_in_dim(gathered, x_index, 0, keepdims=False)
    level_one = own[:, :8].reshape(2, 2, head_size, head_size)
    pair_first = lax.dynamic_index_in_dim(gathered, x_index - x_index % 2, 0, keepdims=False)
    pair_second = lax.dynamic_index_in_dim(gathered, x_index - x_index % 2 + 1, 0, keepdims=False)
    level_two = jnp.stack(
        [pair_first[:, 8:12].reshape(2, 2, 2, quarter, head_size), pair_second[:, 8:12].reshape(2, 2, 2, quarter, head_size)],
        axis=3,
    ).reshape(2, 2, head_size, head_size)
    z_levels = gathered[:, :, 12:].transpose(1, 2, 0, 3, 4).reshape(2, -1, head_size, head_size)
    device_grad = grad_first + level_one[:, 1] + level_two[:, 1] + z_levels[:, -1]
    cross_list = [cross_first, level_one[:, 0], level_two[:, 0]] + [
        z_levels[:, level] for level in range(cross_levels - 3)
    ]
    level_table = bucket_table(per_dev, local_levels)
    local_buckets = jnp.einsum(
        "mji,ihpr->jmhpr", level_table, states, precision=lax.Precision.HIGHEST
    )
    cross_stack = jnp.stack(cross_list)
    cross_buckets = jnp.broadcast_to(cross_stack[None], (per_dev,) + cross_stack.shape)
    buckets = jnp.concatenate([local_buckets, cross_buckets], axis=1).astype(jnp.bfloat16)
    inter_out = jnp.einsum(
        "bthp,bmhpr->bmthr", query_rows, buckets, preferred_element_type=jnp.float32
    )
    output = output + jnp.sum(inter_w * inter_out, axis=1)
    inter_grad = jnp.einsum(
        "bmhpr,bthr->bmthp", buckets, cotan_rows, preferred_element_type=jnp.float32
    )
    grad_query = grad_query + jnp.sum(inter_w * inter_grad, axis=1)
    local_grad = jnp.einsum(
        "mji,jmhpr->ihpr",
        level_table,
        level_grads[:, :local_levels],
        precision=lax.Precision.HIGHEST,
    )
    state_grad = (local_grad + device_grad[None]).astype(jnp.bfloat16)
    grad_key = grad_key + jnp.einsum(
        "buhr,bhpr->buhp", value_rows, state_grad, preferred_element_type=jnp.float32
    )
    grad_value = grad_value + jnp.einsum(
        "buhp,bhpr->buhr", key_rows, state_grad, preferred_element_type=jnp.float32
    )

    def merge_rows(matrix):
        return matrix.reshape(tokens_dev, heads_local * head_size).astype(jnp.bfloat16)

    return (
        merge_rows(output),
        merge_rows(grad_query),
        merge_rows(grad_key),
        merge_rows(grad_value),
    )


def solution(mesh):
    seq_size, head_count = mesh.devices.shape
    split_mesh = Mesh(mesh.devices.reshape(seq_size // 8, 4, 2, head_count), ("z", "x", "core", "head"))
    seq_axes = ("z", "x", "core")
    placed = (
        P(seq_axes + ("head",), None),
        P(seq_axes + ("head",), None),
        P(seq_axes + ("head",), None),
        P(seq_axes + ("head",), None),
        P(None, "head", seq_axes),
    )
    return jax.shard_map(
        body,
        mesh=split_mesh,
        in_specs=placed,
        out_specs=(P(seq_axes, "head"),) * 4,
        check_vma=False,
    )
```

```python
import jax
import jax.numpy as jnp
import numpy as np
from jax import lax
from jax.sharding import Mesh, PartitionSpec as P

SPAN = 256


def swapped(value, axis, distance):
    mask = 2**distance
    pairs = [(source, source ^ mask) for source in range(lax.axis_size(axis))]
    return lax.ppermute(value, axis, pairs)


def bucket_table(per_dev, local_levels):
    level_table = np.zeros((local_levels, per_dev, per_dev), np.float32)
    for level in range(local_levels):
        for target in range(per_dev):
            begin_at = target >> (level + 1) << (level + 1)
            end_at = target >> level << level
            level_table[level, target, begin_at:end_at] = 1.0
    return jnp.asarray(level_table)


def z_table(groups):
    levels = groups.bit_length() - 1
    table = np.zeros((levels, groups, groups), np.float32)
    for level in range(levels):
        for target in range(groups):
            if target >> level & 1:
                table[level, target, target >> (level + 1) << (level + 1) : target >> level << level] = 1.0
    return jnp.asarray(table)


def body(queries, key_vectors, value_vectors, grad_output, level_weights):
    stacked = jnp.stack([queries, key_vectors, value_vectors, grad_output], axis=1)
    exchanged = lax.all_to_all(stacked, "head", split_axis=2, concat_axis=0, tiled=True)
    query_in, key_in, value_in, cotan_in = (exchanged[:, index] for index in range(4))
    tokens_dev = query_in.shape[0]
    heads_local = level_weights.shape[1]
    head_size = query_in.shape[1] // heads_local
    levels_all = level_weights.shape[0]
    per_dev = tokens_dev // SPAN
    local_levels = per_dev.bit_length() - 1
    cross_levels = (lax.axis_size("z") * 8).bit_length() - 1

    def split_spans(matrix):
        return matrix.reshape(per_dev, SPAN, heads_local, head_size)

    query_rows = split_spans(query_in)
    key_rows = split_spans(key_in)
    value_rows = split_spans(value_in)
    cotan_rows = split_spans(cotan_in)
    gain_list = [(head_size * SPAN) ** (-0.5)] + [
        (head_size * 2**tree_level * SPAN) ** (-0.5) for tree_level in range(levels_all - 1)
    ]
    level_gains = jnp.array(gain_list, jnp.float32)
    weights = (level_weights.astype(jnp.float32) / 64.0 * level_gains[:, None, None]).reshape(
        levels_all, heads_local, per_dev, SPAN
    )
    intra_w = jnp.transpose(weights[0], (1, 0, 2))[:, :, :, None]
    inter_w = jnp.transpose(weights[1:], (2, 0, 3, 1))[..., None]
    position = jnp.arange(SPAN, dtype=jnp.int32)
    causal = position[:, None] >= position[None, :]
    scores = jnp.einsum("bthp,buhp->bhtu", query_rows, key_rows, preferred_element_type=jnp.float32)
    attention = jnp.where(causal, scores * intra_w, 0.0).astype(jnp.bfloat16)
    cotan_scores = jnp.einsum(
        "bthr,buhr->bhtu", cotan_rows, value_rows, preferred_element_type=jnp.float32
    )
    grad_scores = jnp.where(causal, cotan_scores * intra_w, 0.0).astype(jnp.bfloat16)
    output = jnp.einsum(
        "bhtu,buhr->bthr", attention, value_rows, preferred_element_type=jnp.float32
    )
    grad_query = jnp.einsum(
        "bhtu,buhp->bthp", grad_scores, key_rows, preferred_element_type=jnp.float32
    )
    grad_key = jnp.einsum(
        "bhtu,bthp->buhp", grad_scores, query_rows, preferred_element_type=jnp.float32
    )
    grad_value = jnp.einsum(
        "bhtu,bthr->buhr", attention, cotan_rows, preferred_element_type=jnp.float32
    )
    states = jnp.einsum("buhp,buhr->bhpr", key_rows, value_rows, preferred_element_type=jnp.float32)
    core_index = lax.axis_index("core")
    x_index = lax.axis_index("x")
    seq_index = (lax.axis_index("z") * 4 + x_index) * 2 + core_index
    upper_bits = (jnp.right_shift(seq_index, jnp.arange(cross_levels, dtype=jnp.int32)) % 2).astype(
        jnp.float32
    )
    weighted = (inter_w * cotan_rows[:, None]).astype(jnp.bfloat16)
    level_grads = jnp.einsum(
        "bthp,bmthr->bmhpr", query_rows, weighted, preferred_element_type=jnp.float32
    )
    running = jnp.sum(states, axis=0)
    pending = jnp.sum(level_grads[:, local_levels:], axis=0) * upper_bits[:, None, None, None]
    packet = jnp.concatenate([running[None], pending], axis=0)
    arrived = swapped(packet, "core", 0)
    cross_first = arrived[0] * upper_bits[0]
    grad_first = (1.0 - upper_bits[0]) * arrived[1]
    running = lax.dynamic_index_in_dim(running + arrived[0], core_index, 0, keepdims=False)
    pending = lax.dynamic_index_in_dim(pending[1:] + arrived[2:], core_index, 1, keepdims=False)
    packet = jnp.concatenate([running[None], pending], axis=0)
    arrived = swapped(packet, "x", 0)
    cross_x1 = arrived[0] * upper_bits[1]
    grad_x1 = (1.0 - upper_bits[1]) * arrived[1]

    def halved(matrix):
        shaped = matrix.reshape(matrix.shape[:-2] + (2, 2, head_size // 4, head_size))
        return lax.dynamic_index_in_dim(shaped, x_index % 2, shaped.ndim - 3, keepdims=False)

    running = halved(running + arrived[0])
    pending = halved(pending[1:] + arrived[2:])
    packet = jnp.concatenate([running[None], pending], axis=0)
    arrived = swapped(packet, "x", 1)
    cross_x2 = arrived[0] * upper_bits[2]
    grad_x2 = (1.0 - upper_bits[2]) * arrived[1]

    def quartered(matrix):
        return lax.dynamic_index_in_dim(matrix, x_index // 2, matrix.ndim - 3, keepdims=False)

    running = quartered(running + arrived[0])
    pending = quartered(pending[1:] + arrived[2:])
    z_rows = lax.dynamic_index_in_dim(z_table(lax.axis_size("z")), lax.axis_index("z"), 1, keepdims=False)
    group_sums = lax.all_gather(running, "z")
    cross_z = jnp.einsum("jb,bpr->jpr", z_rows, group_sums, precision=lax.Precision.HIGHEST)
    contributions = jnp.einsum("jb,jpr->bpr", z_rows, pending, precision=lax.Precision.HIGHEST)
    grad_z = lax.psum_scatter(contributions, "z", scatter_dimension=0, tiled=False)
    own_half = jnp.stack([cross_x2, grad_x2])
    other_half = swapped(own_half, "x", 0)
    even_first = x_index % 2 == 0
    level_two = jnp.stack(
        [jnp.where(even_first, own_half, other_half), jnp.where(even_first, other_half, own_half)], axis=2
    ).reshape(2, head_size, head_size)
    own_levels = jnp.concatenate([jnp.stack([cross_x1, grad_x1]), level_two])
    other_levels = swapped(own_levels, "core", 0)
    core_first = core_index == 0
    near_levels = jnp.stack(
        [jnp.where(core_first, own_levels, other_levels), jnp.where(core_first, other_levels, own_levels)]
    )
    pieces = jnp.concatenate([cross_z, grad_z[None]])
    gathered = lax.all_gather(pieces, ("x", "core")).reshape((4, 2) + pieces.shape)
    z_levels = gathered.transpose(1, 2, 0, 3, 4).reshape(2, -1, head_size, head_size)
    device_grad = grad_first + near_levels[:, 1] + near_levels[:, 3] + z_levels[:, -1]
    cross_list = [cross_first, near_levels[:, 0], near_levels[:, 2]] + [
        z_levels[:, level] for level in range(cross_levels - 3)
    ]
    level_table = bucket_table(per_dev, local_levels)
    local_buckets = jnp.einsum(
        "mji,ihpr->jmhpr", level_table, states, precision=lax.Precision.HIGHEST
    )
    cross_stack = jnp.stack(cross_list)
    cross_buckets = jnp.broadcast_to(cross_stack[None], (per_dev,) + cross_stack.shape)
    buckets = jnp.concatenate([local_buckets, cross_buckets], axis=1).astype(jnp.bfloat16)
    inter_out = jnp.einsum(
        "bthp,bmhpr->bmthr", query_rows, buckets, preferred_element_type=jnp.float32
    )
    output = output + jnp.sum(inter_w * inter_out, axis=1)
    inter_grad = jnp.einsum(
        "bmhpr,bthr->bmthp", buckets, cotan_rows, preferred_element_type=jnp.float32
    )
    grad_query = grad_query + jnp.sum(inter_w * inter_grad, axis=1)
    local_grad = jnp.einsum(
        "mji,jmhpr->ihpr",
        level_table,
        level_grads[:, :local_levels],
        precision=lax.Precision.HIGHEST,
    )
    state_grad = (local_grad + device_grad[None]).astype(jnp.bfloat16)
    grad_key = grad_key + jnp.einsum(
        "buhr,bhpr->buhp", value_rows, state_grad, preferred_element_type=jnp.float32
    )
    grad_value = grad_value + jnp.einsum(
        "buhp,bhpr->buhr", key_rows, state_grad, preferred_element_type=jnp.float32
    )

    def merge_rows(matrix):
        return matrix.reshape(tokens_dev, heads_local * head_size).astype(jnp.bfloat16)

    return (
        merge_rows(output),
        merge_rows(grad_query),
        merge_rows(grad_key),
        merge_rows(grad_value),
    )


def solution(mesh):
    seq_size, head_count = mesh.devices.shape
    split_mesh = Mesh(mesh.devices.reshape(seq_size // 8, 4, 2, head_count), ("z", "x", "core", "head"))
    seq_axes = ("z", "x", "core")
    placed = (
        P(seq_axes + ("head",), None),
        P(seq_axes + ("head",), None),
        P(seq_axes + ("head",), None),
        P(seq_axes + ("head",), None),
        P(None, "head", seq_axes),
    )
    return jax.shard_map(
        body,
        mesh=split_mesh,
        in_specs=placed,
        out_specs=(P(seq_axes, "head"),) * 4,
        check_vma=False,
    )
```

```python
import jax
import jax.numpy as jnp
import numpy as np
from jax import lax
from jax.sharding import Mesh, PartitionSpec as P

SPAN = 256


def swapped(value, axis, distance):
    mask = 2**distance
    pairs = [(source, source ^ mask) for source in range(lax.axis_size(axis))]
    return lax.ppermute(value, axis, pairs)


def bucket_table(per_dev, local_levels):
    level_table = np.zeros((local_levels, per_dev, per_dev), np.float32)
    for level in range(local_levels):
        for target in range(per_dev):
            begin_at = target >> (level + 1) << (level + 1)
            end_at = target >> level << level
            level_table[level, target, begin_at:end_at] = 1.0
    return jnp.asarray(level_table)


def body(queries, key_vectors, value_vectors, grad_output, level_weights):
    stacked = jnp.stack([queries, key_vectors, value_vectors, grad_output], axis=1)
    exchanged = lax.all_to_all(stacked, "head", split_axis=2, concat_axis=0, tiled=True)
    query_in, key_in, value_in, cotan_in = (exchanged[:, index] for index in range(4))
    tokens_dev = query_in.shape[0]
    heads_local = level_weights.shape[1]
    head_size = query_in.shape[1] // heads_local
    levels_all = level_weights.shape[0]
    per_dev = tokens_dev // SPAN
    local_levels = per_dev.bit_length() - 1
    cross_levels = (lax.axis_size("z") * 8).bit_length() - 1

    def split_spans(matrix):
        return matrix.reshape(per_dev, SPAN, heads_local, head_size)

    query_rows = split_spans(query_in)
    key_rows = split_spans(key_in)
    value_rows = split_spans(value_in)
    cotan_rows = split_spans(cotan_in)
    gain_list = [(head_size * SPAN) ** (-0.5)] + [
        (head_size * 2**tree_level * SPAN) ** (-0.5) for tree_level in range(levels_all - 1)
    ]
    level_gains = jnp.array(gain_list, jnp.float32)
    weights = (level_weights.astype(jnp.float32) / 64.0 * level_gains[:, None, None]).reshape(
        levels_all, heads_local, per_dev, SPAN
    )
    intra_w = jnp.transpose(weights[0], (1, 0, 2))[:, :, :, None]
    inter_w = jnp.transpose(weights[1:], (2, 0, 3, 1))[..., None]
    position = jnp.arange(SPAN, dtype=jnp.int32)
    causal = position[:, None] >= position[None, :]
    scores = jnp.einsum("bthp,buhp->bhtu", query_rows, key_rows, preferred_element_type=jnp.float32)
    attention = jnp.where(causal, scores * intra_w, 0.0).astype(jnp.bfloat16)
    cotan_scores = jnp.einsum(
        "bthr,buhr->bhtu", cotan_rows, value_rows, preferred_element_type=jnp.float32
    )
    grad_scores = jnp.where(causal, cotan_scores * intra_w, 0.0).astype(jnp.bfloat16)
    output = jnp.einsum(
        "bhtu,buhr->bthr", attention, value_rows, preferred_element_type=jnp.float32
    )
    grad_query = jnp.einsum(
        "bhtu,buhp->bthp", grad_scores, key_rows, preferred_element_type=jnp.float32
    )
    grad_key = jnp.einsum(
        "bhtu,bthp->buhp", grad_scores, query_rows, preferred_element_type=jnp.float32
    )
    grad_value = jnp.einsum(
        "bhtu,bthr->buhr", attention, cotan_rows, preferred_element_type=jnp.float32
    )
    states = jnp.einsum("buhp,buhr->bhpr", key_rows, value_rows, preferred_element_type=jnp.float32)
    core_index = lax.axis_index("core")
    x_index = lax.axis_index("x")
    seq_index = (lax.axis_index("z") * 4 + x_index) * 2 + core_index
    upper_bits = (jnp.right_shift(seq_index, jnp.arange(cross_levels, dtype=jnp.int32)) % 2).astype(
        jnp.float32
    )
    weighted = (inter_w * cotan_rows[:, None]).astype(jnp.bfloat16)
    level_grads = jnp.einsum(
        "bthp,bmthr->bmhpr", query_rows, weighted, preferred_element_type=jnp.float32
    )
    running = jnp.sum(states, axis=0)
    pending = jnp.sum(level_grads[:, local_levels:], axis=0) * upper_bits[:, None, None, None]
    packet = jnp.concatenate([running[None], pending], axis=0)
    arrived = swapped(packet, "core", 0)
    cross_first = arrived[0] * upper_bits[0]
    grad_first = (1.0 - upper_bits[0]) * arrived[1]
    running = lax.dynamic_index_in_dim(running + arrived[0], core_index, 0, keepdims=False)
    pending = lax.dynamic_index_in_dim(pending[1:] + arrived[2:], core_index, 1, keepdims=False)
    packet = jnp.concatenate([running[None], pending], axis=0)
    arrived = swapped(packet, "x", 0)
    cross_x1 = arrived[0] * upper_bits[1]
    grad_x1 = (1.0 - upper_bits[1]) * arrived[1]

    def halved(matrix):
        shaped = matrix.reshape(matrix.shape[:-2] + (2, 2, head_size // 4, head_size))
        return lax.dynamic_index_in_dim(shaped, x_index % 2, shaped.ndim - 3, keepdims=False)

    running = halved(running + arrived[0])
    pending = halved(pending[1:] + arrived[2:])
    packet = jnp.concatenate([running[None], pending], axis=0)
    arrived = swapped(packet, "x", 1)
    cross_x2 = arrived[0] * upper_bits[2]
    grad_x2 = (1.0 - upper_bits[2]) * arrived[1]

    def quartered(matrix):
        return lax.dynamic_index_in_dim(matrix, x_index // 2, matrix.ndim - 3, keepdims=False)

    running = quartered(running + arrived[0])
    pending = quartered(pending[1:] + arrived[2:])
    grad_z = jnp.zeros_like(running)
    cross_z = []
    for z_bit in range(cross_levels - 3):
        tree_bit = z_bit + 3
        packet = jnp.concatenate([running[None], pending], axis=0)
        arrived = swapped(packet, "z", z_bit)
        cross_z.append(arrived[0] * upper_bits[tree_bit])
        grad_z = grad_z + (1.0 - upper_bits[tree_bit]) * arrived[1]
        running = running + arrived[0]
        pending = pending[1:] + arrived[2:]

    z_part = jnp.concatenate([jnp.stack(cross_z), grad_z[None]])
    odd_x = x_index % 2 == 1
    high_x = x_index // 2 == 1
    pair_part = swapped(jnp.concatenate([z_part, jnp.stack([cross_x2, grad_x2]).reshape(-1, head_size // 4, head_size)]), "x", 0)
    z_levels = z_part.shape[0]

    def ordered(own, other, other_first):
        return jnp.stack([jnp.where(other_first, other, own), jnp.where(other_first, own, other)])

    z_half = ordered(z_part, pair_part[:z_levels], odd_x)
    level_two = ordered(jnp.stack([cross_x2, grad_x2]), pair_part[z_levels:].reshape(2, 2, head_size // 4, head_size), odd_x)
    level_two = level_two.transpose(1, 2, 0, 3, 4).reshape(2, head_size, head_size)
    z_full = ordered(z_half, swapped(z_half, "x", 1), high_x)
    z_full = z_full.transpose(2, 0, 1, 3, 4).reshape(z_levels, head_size, head_size)
    own_levels = jnp.concatenate([jnp.stack([cross_x1, grad_x1]), level_two, z_full])
    both_heads = ordered(own_levels, swapped(own_levels, "core", 0), core_index == 1)
    device_grad = grad_first + both_heads[:, 1] + both_heads[:, 3] + both_heads[:, -1]
    cross_list = [cross_first, both_heads[:, 0], both_heads[:, 2]] + [
        both_heads[:, 4 + level] for level in range(cross_levels - 3)
    ]
    level_table = bucket_table(per_dev, local_levels)
    local_buckets = jnp.einsum(
        "mji,ihpr->jmhpr", level_table, states, precision=lax.Precision.HIGHEST
    )
    cross_stack = jnp.stack(cross_list)
    cross_buckets = jnp.broadcast_to(cross_stack[None], (per_dev,) + cross_stack.shape)
    buckets = jnp.concatenate([local_buckets, cross_buckets], axis=1).astype(jnp.bfloat16)
    inter_out = jnp.einsum(
        "bthp,bmhpr->bmthr", query_rows, buckets, preferred_element_type=jnp.float32
    )
    output = output + jnp.sum(inter_w * inter_out, axis=1)
    inter_grad = jnp.einsum(
        "bmhpr,bthr->bmthp", buckets, cotan_rows, preferred_element_type=jnp.float32
    )
    grad_query = grad_query + jnp.sum(inter_w * inter_grad, axis=1)
    local_grad = jnp.einsum(
        "mji,jmhpr->ihpr",
        level_table,
        level_grads[:, :local_levels],
        precision=lax.Precision.HIGHEST,
    )
    state_grad = (local_grad + device_grad[None]).astype(jnp.bfloat16)
    grad_key = grad_key + jnp.einsum(
        "buhr,bhpr->buhp", value_rows, state_grad, preferred_element_type=jnp.float32
    )
    grad_value = grad_value + jnp.einsum(
        "buhp,bhpr->buhr", key_rows, state_grad, preferred_element_type=jnp.float32
    )

    def merge_rows(matrix):
        return matrix.reshape(tokens_dev, heads_local * head_size).astype(jnp.bfloat16)

    return (
        merge_rows(output),
        merge_rows(grad_query),
        merge_rows(grad_key),
        merge_rows(grad_value),
    )


def solution(mesh):
    seq_size, head_count = mesh.devices.shape
    split_mesh = Mesh(mesh.devices.reshape(seq_size // 8, 4, 2, head_count), ("z", "x", "core", "head"))
    seq_axes = ("z", "x", "core")
    placed = (
        P(seq_axes + ("head",), None),
        P(seq_axes + ("head",), None),
        P(seq_axes + ("head",), None),
        P(seq_axes + ("head",), None),
        P(None, "head", seq_axes),
    )
    return jax.shard_map(
        body,
        mesh=split_mesh,
        in_specs=placed,
        out_specs=(P(seq_axes, "head"),) * 4,
        check_vma=False,
    )
```

```python
import jax
import jax.numpy as jnp
import numpy as np
from jax import lax
from jax.sharding import Mesh, PartitionSpec as P

SPAN = 256


def swapped(value, axis, distance):
    mask = 2**distance
    pairs = [(source, source ^ mask) for source in range(lax.axis_size(axis))]
    return lax.ppermute(value, axis, pairs)


def bucket_table(per_dev, local_levels):
    level_table = np.zeros((local_levels, per_dev, per_dev), np.float32)
    for level in range(local_levels):
        for target in range(per_dev):
            begin_at = target >> (level + 1) << (level + 1)
            end_at = target >> level << level
            level_table[level, target, begin_at:end_at] = 1.0
    return jnp.asarray(level_table)


def z_tables(groups):
    levels = groups.bit_length() - 1
    choice = np.zeros((groups, groups), np.int32)
    forward_table = np.zeros((groups, levels, groups), np.float32)
    backward_table = np.zeros((groups, groups), np.float32)
    for own in range(groups):
        for other in range(groups):
            if other == own:
                continue
            level = (own ^ other).bit_length() - 1
            choice[own, other] = 1 if other > own else 2 + level
            if other < own:
                forward_table[own, level, other] = 1.0
            else:
                backward_table[own, other] = 1.0
    return jnp.asarray(choice), jnp.asarray(forward_table), jnp.asarray(backward_table)


def body(queries, key_vectors, value_vectors, grad_output, level_weights):
    stacked = jnp.stack([queries, key_vectors, value_vectors, grad_output], axis=1)
    exchanged = lax.all_to_all(stacked, "head", split_axis=2, concat_axis=0, tiled=True)
    query_in, key_in, value_in, cotan_in = (exchanged[:, index] for index in range(4))
    tokens_dev = query_in.shape[0]
    heads_local = level_weights.shape[1]
    head_size = query_in.shape[1] // heads_local
    levels_all = level_weights.shape[0]
    per_dev = tokens_dev // SPAN
    local_levels = per_dev.bit_length() - 1
    cross_levels = (lax.axis_size("z") * 8).bit_length() - 1

    def split_spans(matrix):
        return matrix.reshape(per_dev, SPAN, heads_local, head_size)

    query_rows = split_spans(query_in)
    key_rows = split_spans(key_in)
    value_rows = split_spans(value_in)
    cotan_rows = split_spans(cotan_in)
    gain_list = [(head_size * SPAN) ** (-0.5)] + [
        (head_size * 2**tree_level * SPAN) ** (-0.5) for tree_level in range(levels_all - 1)
    ]
    level_gains = jnp.array(gain_list, jnp.float32)
    weights = (level_weights.astype(jnp.float32) / 64.0 * level_gains[:, None, None]).reshape(
        levels_all, heads_local, per_dev, SPAN
    )
    intra_w = jnp.transpose(weights[0], (1, 0, 2))[:, :, :, None]
    inter_w = jnp.transpose(weights[1:], (2, 0, 3, 1))[..., None]
    position = jnp.arange(SPAN, dtype=jnp.int32)
    causal = position[:, None] >= position[None, :]
    scores = jnp.einsum("bthp,buhp->bhtu", query_rows, key_rows, preferred_element_type=jnp.float32)
    attention = jnp.where(causal, scores * intra_w, 0.0).astype(jnp.bfloat16)
    cotan_scores = jnp.einsum(
        "bthr,buhr->bhtu", cotan_rows, value_rows, preferred_element_type=jnp.float32
    )
    grad_scores = jnp.where(causal, cotan_scores * intra_w, 0.0).astype(jnp.bfloat16)
    output = jnp.einsum(
        "bhtu,buhr->bthr", attention, value_rows, preferred_element_type=jnp.float32
    )
    grad_query = jnp.einsum(
        "bhtu,buhp->bthp", grad_scores, key_rows, preferred_element_type=jnp.float32
    )
    grad_key = jnp.einsum(
        "bhtu,bthp->buhp", grad_scores, query_rows, preferred_element_type=jnp.float32
    )
    grad_value = jnp.einsum(
        "bhtu,bthr->buhr", attention, cotan_rows, preferred_element_type=jnp.float32
    )
    states = jnp.einsum("buhp,buhr->bhpr", key_rows, value_rows, preferred_element_type=jnp.float32)
    core_index = lax.axis_index("core")
    x_index = lax.axis_index("x")
    seq_index = (lax.axis_index("z") * 4 + x_index) * 2 + core_index
    upper_bits = (jnp.right_shift(seq_index, jnp.arange(cross_levels, dtype=jnp.int32)) % 2).astype(
        jnp.float32
    )
    weighted = (inter_w * cotan_rows[:, None]).astype(jnp.bfloat16)
    level_grads = jnp.einsum(
        "bthp,bmthr->bmhpr", query_rows, weighted, preferred_element_type=jnp.float32
    )
    running = jnp.sum(states, axis=0)
    pending = jnp.sum(level_grads[:, local_levels:], axis=0) * upper_bits[:, None, None, None]
    packet = jnp.concatenate([running[None], pending], axis=0)
    arrived = swapped(packet, "core", 0)
    cross_first = arrived[0] * upper_bits[0]
    grad_first = (1.0 - upper_bits[0]) * arrived[1]
    running = lax.dynamic_index_in_dim(running + arrived[0], core_index, 0, keepdims=False)
    pending = lax.dynamic_index_in_dim(pending[1:] + arrived[2:], core_index, 1, keepdims=False)
    packet = jnp.concatenate([running[None], pending], axis=0)
    arrived = swapped(packet, "x", 0)
    cross_x1 = arrived[0] * upper_bits[1]
    grad_x1 = (1.0 - upper_bits[1]) * arrived[1]

    def halved(matrix):
        shaped = matrix.reshape(matrix.shape[:-2] + (2, 2, head_size // 4, head_size))
        return lax.dynamic_index_in_dim(shaped, x_index % 2, shaped.ndim - 3, keepdims=False)

    running = halved(running + arrived[0])
    pending = halved(pending[1:] + arrived[2:])
    packet = jnp.concatenate([running[None], pending], axis=0)
    arrived = swapped(packet, "x", 1)
    cross_x2 = arrived[0] * upper_bits[2]
    grad_x2 = (1.0 - upper_bits[2]) * arrived[1]

    def quartered(matrix):
        return lax.dynamic_index_in_dim(matrix, x_index // 2, matrix.ndim - 3, keepdims=False)

    running = quartered(running + arrived[0])
    pending = quartered(pending[1:] + arrived[2:])
    z_count = lax.axis_size("z")
    z_index = lax.axis_index("z")
    choice, forward_table, backward_table = z_tables(z_count)
    options = jnp.concatenate([jnp.zeros_like(running)[None], running[None], pending])
    chunks = jnp.take(options, lax.dynamic_index_in_dim(choice, z_index, 0, keepdims=False), axis=0)
    received = lax.all_to_all(chunks, "z", 0, 0, tiled=True)
    forward_rows = lax.dynamic_index_in_dim(forward_table, z_index, 0, keepdims=False)
    backward_row = lax.dynamic_index_in_dim(backward_table, z_index, 0, keepdims=False)
    cross_z = list(jnp.einsum("jg,gpr->jpr", forward_rows, received, precision=lax.Precision.HIGHEST))
    grad_z = jnp.einsum("g,gpr->pr", backward_row, received, precision=lax.Precision.HIGHEST)
    z_part = jnp.concatenate([jnp.stack(cross_z), grad_z[None]])
    odd_x = x_index % 2 == 1
    high_x = x_index // 2 == 1
    pair_part = swapped(jnp.concatenate([z_part, jnp.stack([cross_x2, grad_x2]).reshape(-1, head_size // 4, head_size)]), "x", 0)
    z_levels = z_part.shape[0]

    def ordered(own, other, other_first):
        return jnp.stack([jnp.where(other_first, other, own), jnp.where(other_first, own, other)])

    z_half = ordered(z_part, pair_part[:z_levels], odd_x)
    level_two = ordered(jnp.stack([cross_x2, grad_x2]), pair_part[z_levels:].reshape(2, 2, head_size // 4, head_size), odd_x)
    level_two = level_two.transpose(1, 2, 0, 3, 4).reshape(2, head_size, head_size)
    z_full = ordered(z_half, swapped(z_half, "x", 1), high_x)
    z_full = z_full.transpose(2, 0, 1, 3, 4).reshape(z_levels, head_size, head_size)
    own_levels = jnp.concatenate([jnp.stack([cross_x1, grad_x1]), level_two, z_full])
    both_heads = ordered(own_levels, swapped(own_levels, "core", 0), core_index == 1)
    device_grad = grad_first + both_heads[:, 1] + both_heads[:, 3] + both_heads[:, -1]
    cross_list = [cross_first, both_heads[:, 0], both_heads[:, 2]] + [
        both_heads[:, 4 + level] for level in range(cross_levels - 3)
    ]
    level_table = bucket_table(per_dev, local_levels)
    local_buckets = jnp.einsum(
        "mji,ihpr->jmhpr", level_table, states, precision=lax.Precision.HIGHEST
    )
    cross_stack = jnp.stack(cross_list)
    cross_buckets = jnp.broadcast_to(cross_stack[None], (per_dev,) + cross_stack.shape)
    buckets = jnp.concatenate([local_buckets, cross_buckets], axis=1).astype(jnp.bfloat16)
    inter_out = jnp.einsum(
        "bthp,bmhpr->bmthr", query_rows, buckets, preferred_element_type=jnp.float32
    )
    output = output + jnp.sum(inter_w * inter_out, axis=1)
    inter_grad = jnp.einsum(
        "bmhpr,bthr->bmthp", buckets, cotan_rows, preferred_element_type=jnp.float32
    )
    grad_query = grad_query + jnp.sum(inter_w * inter_grad, axis=1)
    local_grad = jnp.einsum(
        "mji,jmhpr->ihpr",
        level_table,
        level_grads[:, :local_levels],
        precision=lax.Precision.HIGHEST,
    )
    state_grad = (local_grad + device_grad[None]).astype(jnp.bfloat16)
    grad_key = grad_key + jnp.einsum(
        "buhr,bhpr->buhp", value_rows, state_grad, preferred_element_type=jnp.float32
    )
    grad_value = grad_value + jnp.einsum(
        "buhp,bhpr->buhr", key_rows, state_grad, preferred_element_type=jnp.float32
    )

    def merge_rows(matrix):
        return matrix.reshape(tokens_dev, heads_local * head_size).astype(jnp.bfloat16)

    return (
        merge_rows(output),
        merge_rows(grad_query),
        merge_rows(grad_key),
        merge_rows(grad_value),
    )


def solution(mesh):
    seq_size, head_count = mesh.devices.shape
    split_mesh = Mesh(mesh.devices.reshape(seq_size // 8, 4, 2, head_count), ("z", "x", "core", "head"))
    seq_axes = ("z", "x", "core")
    placed = (
        P(seq_axes + ("head",), None),
        P(seq_axes + ("head",), None),
        P(seq_axes + ("head",), None),
        P(seq_axes + ("head",), None),
        P(None, "head", seq_axes),
    )
    return jax.shard_map(
        body,
        mesh=split_mesh,
        in_specs=placed,
        out_specs=(P(seq_axes, "head"),) * 4,
        check_vma=False,
    )
```

```python
import jax
import jax.numpy as jnp
import numpy as np
from jax import lax
from jax.sharding import Mesh, PartitionSpec as P

SPAN = 256


def swapped(value, axis, distance):
    mask = 2**distance
    pairs = [(source, source ^ mask) for source in range(lax.axis_size(axis))]
    return lax.ppermute(value, axis, pairs)


def bucket_table(per_dev, local_levels):
    level_table = np.zeros((local_levels, per_dev, per_dev), np.float32)
    for level in range(local_levels):
        for target in range(per_dev):
            begin_at = target >> (level + 1) << (level + 1)
            end_at = target >> level << level
            level_table[level, target, begin_at:end_at] = 1.0
    return jnp.asarray(level_table)


def z_tables(groups):
    levels = groups.bit_length() - 1
    choice = np.zeros((groups, groups), np.int32)
    forward_table = np.zeros((groups, levels, groups), np.float32)
    backward_table = np.zeros((groups, groups), np.float32)
    for own in range(groups):
        for other in range(groups):
            if other == own:
                continue
            level = (own ^ other).bit_length() - 1
            choice[own, other] = 1 if other > own else 2 + level
            if other < own:
                forward_table[own, level, other] = 1.0
            else:
                backward_table[own, other] = 1.0
    return jnp.asarray(choice), jnp.asarray(forward_table), jnp.asarray(backward_table)


def body(queries, key_vectors, value_vectors, grad_output, level_weights):
    stacked = jnp.stack([queries, key_vectors, value_vectors, grad_output], axis=1)
    exchanged = lax.all_to_all(stacked, "head", split_axis=2, concat_axis=0, tiled=True)
    query_in, key_in, value_in, cotan_in = (exchanged[:, index] for index in range(4))
    tokens_dev = query_in.shape[0]
    heads_local = level_weights.shape[1]
    head_size = query_in.shape[1] // heads_local
    levels_all = level_weights.shape[0]
    per_dev = tokens_dev // SPAN
    local_levels = per_dev.bit_length() - 1
    cross_levels = (lax.axis_size("z") * 8).bit_length() - 1

    def split_spans(matrix):
        return matrix.reshape(per_dev, SPAN, heads_local, head_size)

    query_rows = split_spans(query_in)
    key_rows = split_spans(key_in)
    value_rows = split_spans(value_in)
    cotan_rows = split_spans(cotan_in)
    gain_list = [(head_size * SPAN) ** (-0.5)] + [
        (head_size * 2**tree_level * SPAN) ** (-0.5) for tree_level in range(levels_all - 1)
    ]
    level_gains = jnp.array(gain_list, jnp.float32)
    weights = (level_weights.astype(jnp.float32) / 64.0 * level_gains[:, None, None]).reshape(
        levels_all, heads_local, per_dev, SPAN
    )
    intra_w = jnp.transpose(weights[0], (1, 0, 2))[:, :, :, None]
    inter_w = jnp.transpose(weights[1:], (2, 0, 3, 1))[..., None]
    position = jnp.arange(SPAN, dtype=jnp.int32)
    causal = position[:, None] >= position[None, :]
    scores = jnp.einsum("bthp,buhp->bhtu", query_rows, key_rows, preferred_element_type=jnp.float32)
    attention = jnp.where(causal, scores * intra_w, 0.0).astype(jnp.bfloat16)
    cotan_scores = jnp.einsum(
        "bthr,buhr->bhtu", cotan_rows, value_rows, preferred_element_type=jnp.float32
    )
    grad_scores = jnp.where(causal, cotan_scores * intra_w, 0.0).astype(jnp.bfloat16)
    output = jnp.einsum(
        "bhtu,buhr->bthr", attention, value_rows, preferred_element_type=jnp.float32
    )
    grad_query = jnp.einsum(
        "bhtu,buhp->bthp", grad_scores, key_rows, preferred_element_type=jnp.float32
    )
    grad_key = jnp.einsum(
        "bhtu,bthp->buhp", grad_scores, query_rows, preferred_element_type=jnp.float32
    )
    grad_value = jnp.einsum(
        "bhtu,bthr->buhr", attention, cotan_rows, preferred_element_type=jnp.float32
    )
    states = jnp.einsum("buhp,buhr->bhpr", key_rows, value_rows, preferred_element_type=jnp.float32)
    core_index = lax.axis_index("core")
    x_index = lax.axis_index("x")
    seq_index = (lax.axis_index("z") * 4 + x_index) * 2 + core_index
    upper_bits = (jnp.right_shift(seq_index, jnp.arange(cross_levels, dtype=jnp.int32)) % 2).astype(
        jnp.float32
    )
    weighted = (inter_w * cotan_rows[:, None]).astype(jnp.bfloat16)
    level_grads = jnp.einsum(
        "bthp,bmthr->bmhpr", query_rows, weighted, preferred_element_type=jnp.float32
    )
    running = jnp.sum(states, axis=0)
    pending = jnp.sum(level_grads[:, local_levels:], axis=0) * upper_bits[:, None, None, None]
    packet = jnp.concatenate([running[None], pending], axis=0)
    arrived = swapped(packet, "core", 0)
    cross_first = arrived[0] * upper_bits[0]
    grad_first = (1.0 - upper_bits[0]) * arrived[1]
    running = lax.dynamic_index_in_dim(running + arrived[0], core_index, 0, keepdims=False)
    pending = lax.dynamic_index_in_dim(pending[1:] + arrived[2:], core_index, 1, keepdims=False)
    packet = jnp.concatenate([running[None], pending], axis=0)
    arrived = swapped(packet, "x", 0)
    cross_x1 = arrived[0] * upper_bits[1]
    grad_x1 = (1.0 - upper_bits[1]) * arrived[1]

    def halved(matrix):
        shaped = matrix.reshape(matrix.shape[:-2] + (2, 2, head_size // 4, head_size))
        return lax.dynamic_index_in_dim(shaped, x_index % 2, shaped.ndim - 3, keepdims=False)

    running = halved(running + arrived[0])
    pending = halved(pending[1:] + arrived[2:])
    packet = jnp.concatenate([running[None], pending], axis=0)
    arrived = swapped(packet, "x", 1)
    cross_x2 = arrived[0] * upper_bits[2]
    grad_x2 = (1.0 - upper_bits[2]) * arrived[1]

    def quartered(matrix):
        return lax.dynamic_index_in_dim(matrix, x_index // 2, matrix.ndim - 3, keepdims=False)

    running = quartered(running + arrived[0])
    pending = quartered(pending[1:] + arrived[2:])
    z_count = lax.axis_size("z")
    z_index = lax.axis_index("z")
    choice, forward_table, backward_table = z_tables(z_count)
    options = jnp.concatenate([jnp.zeros_like(running)[None], running[None], pending])
    chunks = jnp.take(options, lax.dynamic_index_in_dim(choice, z_index, 0, keepdims=False), axis=0)
    received = lax.all_to_all(chunks, "z", 0, 0, tiled=True)
    forward_rows = lax.dynamic_index_in_dim(forward_table, z_index, 0, keepdims=False)
    backward_row = lax.dynamic_index_in_dim(backward_table, z_index, 0, keepdims=False)
    cross_z = list(jnp.einsum("jg,gpr->jpr", forward_rows, received, precision=lax.Precision.HIGHEST))
    grad_z = jnp.einsum("g,gpr->pr", backward_row, received, precision=lax.Precision.HIGHEST)
    odd_x = x_index % 2 == 1

    def ordered(own, other, other_first):
        return jnp.stack([jnp.where(other_first, other, own), jnp.where(other_first, own, other)])

    half_two = jnp.stack([cross_x2, grad_x2])
    level_two = ordered(half_two, swapped(half_two, "x", 0), odd_x)
    level_two = level_two.transpose(1, 2, 0, 3, 4).reshape(2, head_size, head_size)
    own_levels = jnp.concatenate([jnp.stack([cross_x1, grad_x1]), level_two])
    near_levels = ordered(own_levels, swapped(own_levels, "core", 0), core_index == 1)
    z_part = jnp.concatenate([jnp.stack(cross_z), grad_z[None]])
    spread = jnp.broadcast_to(z_part[None], (8,) + z_part.shape)
    z_levels = lax.all_to_all(spread, ("x", "core"), 0, 0, tiled=True).reshape((4, 2) + z_part.shape)
    z_levels = z_levels.transpose(1, 2, 0, 3, 4).reshape(2, z_part.shape[0], head_size, head_size)
    device_grad = grad_first + near_levels[:, 1] + near_levels[:, 3] + z_levels[:, -1]
    cross_list = [cross_first, near_levels[:, 0], near_levels[:, 2]] + [
        z_levels[:, level] for level in range(cross_levels - 3)
    ]
    level_table = bucket_table(per_dev, local_levels)
    local_buckets = jnp.einsum(
        "mji,ihpr->jmhpr", level_table, states, precision=lax.Precision.HIGHEST
    )
    cross_stack = jnp.stack(cross_list)
    cross_buckets = jnp.broadcast_to(cross_stack[None], (per_dev,) + cross_stack.shape)
    buckets = jnp.concatenate([local_buckets, cross_buckets], axis=1).astype(jnp.bfloat16)
    inter_out = jnp.einsum(
        "bthp,bmhpr->bmthr", query_rows, buckets, preferred_element_type=jnp.float32
    )
    output = output + jnp.sum(inter_w * inter_out, axis=1)
    inter_grad = jnp.einsum(
        "bmhpr,bthr->bmthp", buckets, cotan_rows, preferred_element_type=jnp.float32
    )
    grad_query = grad_query + jnp.sum(inter_w * inter_grad, axis=1)
    local_grad = jnp.einsum(
        "mji,jmhpr->ihpr",
        level_table,
        level_grads[:, :local_levels],
        precision=lax.Precision.HIGHEST,
    )
    state_grad = (local_grad + device_grad[None]).astype(jnp.bfloat16)
    grad_key = grad_key + jnp.einsum(
        "buhr,bhpr->buhp", value_rows, state_grad, preferred_element_type=jnp.float32
    )
    grad_value = grad_value + jnp.einsum(
        "buhp,bhpr->buhr", key_rows, state_grad, preferred_element_type=jnp.float32
    )

    def merge_rows(matrix):
        return matrix.reshape(tokens_dev, heads_local * head_size).astype(jnp.bfloat16)

    return (
        merge_rows(output),
        merge_rows(grad_query),
        merge_rows(grad_key),
        merge_rows(grad_value),
    )


def solution(mesh):
    seq_size, head_count = mesh.devices.shape
    split_mesh = Mesh(mesh.devices.reshape(seq_size // 8, 4, 2, head_count), ("z", "x", "core", "head"))
    seq_axes = ("z", "x", "core")
    placed = (
        P(seq_axes + ("head",), None),
        P(seq_axes + ("head",), None),
        P(seq_axes + ("head",), None),
        P(seq_axes + ("head",), None),
        P(None, "head", seq_axes),
    )
    return jax.shard_map(
        body,
        mesh=split_mesh,
        in_specs=placed,
        out_specs=(P(seq_axes, "head"),) * 4,
        check_vma=False,
    )
```

```python
import jax
import jax.numpy as jnp
import numpy as np
from jax import lax
from jax.sharding import Mesh, PartitionSpec as P

SPAN = 256


def swapped(value, axis, distance):
    mask = 2**distance
    pairs = [(source, source ^ mask) for source in range(lax.axis_size(axis))]
    return lax.ppermute(value, axis, pairs)


def bucket_table(per_dev, local_levels):
    level_table = np.zeros((local_levels, per_dev, per_dev), np.float32)
    for level in range(local_levels):
        for target in range(per_dev):
            begin_at = target >> (level + 1) << (level + 1)
            end_at = target >> level << level
            level_table[level, target, begin_at:end_at] = 1.0
    return jnp.asarray(level_table)


def z_tables(groups):
    levels = groups.bit_length() - 1
    choice = np.zeros((groups, groups), np.int32)
    forward_table = np.zeros((groups, levels, groups), np.float32)
    backward_table = np.zeros((groups, groups), np.float32)
    for own in range(groups):
        for other in range(groups):
            if other == own:
                continue
            level = (own ^ other).bit_length() - 1
            choice[own, other] = 1 if other > own else 2 + level
            if other < own:
                forward_table[own, level, other] = 1.0
            else:
                backward_table[own, other] = 1.0
    return jnp.asarray(choice), jnp.asarray(forward_table), jnp.asarray(backward_table)


def body(queries, key_vectors, value_vectors, grad_output, level_weights):
    stacked = jnp.stack([queries, key_vectors, value_vectors, grad_output], axis=1)
    exchanged = lax.all_to_all(stacked, "head", split_axis=2, concat_axis=0, tiled=True)
    query_in, key_in, value_in, cotan_in = (exchanged[:, index] for index in range(4))
    tokens_dev = query_in.shape[0]
    heads_local = level_weights.shape[1]
    head_size = query_in.shape[1] // heads_local
    levels_all = level_weights.shape[0]
    per_dev = tokens_dev // SPAN
    local_levels = per_dev.bit_length() - 1
    cross_levels = (lax.axis_size("z") * 8).bit_length() - 1

    def split_spans(matrix):
        return matrix.reshape(per_dev, SPAN, heads_local, head_size)

    query_rows = split_spans(query_in)
    key_rows = split_spans(key_in)
    value_rows = split_spans(value_in)
    cotan_rows = split_spans(cotan_in)
    gain_list = [(head_size * SPAN) ** (-0.5)] + [
        (head_size * 2**tree_level * SPAN) ** (-0.5) for tree_level in range(levels_all - 1)
    ]
    level_gains = jnp.array(gain_list, jnp.float32)
    weights = (level_weights.astype(jnp.float32) / 64.0 * level_gains[:, None, None]).reshape(
        levels_all, heads_local, per_dev, SPAN
    )
    intra_w = jnp.transpose(weights[0], (1, 0, 2))[:, :, :, None]
    inter_w = jnp.transpose(weights[1:], (2, 0, 3, 1))[..., None]
    position = jnp.arange(SPAN, dtype=jnp.int32)
    causal = position[:, None] >= position[None, :]
    scores = jnp.einsum("bthp,buhp->bhtu", query_rows, key_rows, preferred_element_type=jnp.float32)
    attention = jnp.where(causal, scores * intra_w, 0.0).astype(jnp.bfloat16)
    cotan_scores = jnp.einsum(
        "bthr,buhr->bhtu", cotan_rows, value_rows, preferred_element_type=jnp.float32
    )
    grad_scores = jnp.where(causal, cotan_scores * intra_w, 0.0).astype(jnp.bfloat16)
    output = jnp.einsum(
        "bhtu,buhr->bthr", attention, value_rows, preferred_element_type=jnp.float32
    )
    grad_query = jnp.einsum(
        "bhtu,buhp->bthp", grad_scores, key_rows, preferred_element_type=jnp.float32
    )
    grad_key = jnp.einsum(
        "bhtu,bthp->buhp", grad_scores, query_rows, preferred_element_type=jnp.float32
    )
    grad_value = jnp.einsum(
        "bhtu,bthr->buhr", attention, cotan_rows, preferred_element_type=jnp.float32
    )
    states = jnp.einsum("buhp,buhr->bhpr", key_rows, value_rows, preferred_element_type=jnp.float32)
    core_index = lax.axis_index("core")
    x_index = lax.axis_index("x")
    seq_index = (lax.axis_index("z") * 4 + x_index) * 2 + core_index
    upper_bits = (jnp.right_shift(seq_index, jnp.arange(cross_levels, dtype=jnp.int32)) % 2).astype(
        jnp.float32
    )
    weighted = (inter_w * cotan_rows[:, None]).astype(jnp.bfloat16)
    level_grads = jnp.einsum(
        "bthp,bmthr->bmhpr", query_rows, weighted, preferred_element_type=jnp.float32
    )
    running = jnp.sum(states, axis=0)
    pending = jnp.sum(level_grads[:, local_levels:], axis=0) * upper_bits[:, None, None, None]
    packet = jnp.concatenate([running[None], pending], axis=0)
    arrived = swapped(packet, "core", 0)
    cross_first = arrived[0] * upper_bits[0]
    grad_first = (1.0 - upper_bits[0]) * arrived[1]
    running = lax.dynamic_index_in_dim(running + arrived[0], core_index, 0, keepdims=False)
    pending = lax.dynamic_index_in_dim(pending[1:] + arrived[2:], core_index, 1, keepdims=False)
    quarter = head_size // 4
    x_choice, x_forward, x_backward = z_tables(lax.axis_size("x"))
    x_options = jnp.concatenate([jnp.zeros_like(running)[None], running[None], pending[:2]])
    near_chunks = jnp.take(x_options, lax.dynamic_index_in_dim(x_choice, x_index, 0, keepdims=False), axis=0)
    far_chunks = jnp.concatenate([running[None], pending[2:]]).reshape(-1, 4, quarter, head_size)
    x_send = jnp.concatenate([near_chunks.reshape(4, 4, quarter, head_size), far_chunks.transpose(1, 0, 2, 3)], axis=1)
    x_received = lax.all_to_all(x_send, "x", 0, 0, tiled=True)
    near_received = x_received[:, :4].reshape(4, head_size, head_size)
    cross_x = jnp.einsum(
        "jg,gpr->jpr",
        lax.dynamic_index_in_dim(x_forward, x_index, 0, keepdims=False),
        near_received,
        precision=lax.Precision.HIGHEST,
    )
    grad_x = jnp.einsum(
        "g,gpr->pr",
        lax.dynamic_index_in_dim(x_backward, x_index, 0, keepdims=False),
        near_received,
        precision=lax.Precision.HIGHEST,
    )
    far_received = jnp.sum(x_received[:, 4:], axis=0)
    running = far_received[0]
    pending = far_received[1:]
    z_count = lax.axis_size("z")
    z_index = lax.axis_index("z")
    choice, forward_table, backward_table = z_tables(z_count)
    options = jnp.concatenate([jnp.zeros_like(running)[None], running[None], pending])
    chunks = jnp.take(options, lax.dynamic_index_in_dim(choice, z_index, 0, keepdims=False), axis=0)
    received = lax.all_to_all(chunks, "z", 0, 0, tiled=True)
    forward_rows = lax.dynamic_index_in_dim(forward_table, z_index, 0, keepdims=False)
    backward_row = lax.dynamic_index_in_dim(backward_table, z_index, 0, keepdims=False)
    cross_z = list(jnp.einsum("jg,gpr->jpr", forward_rows, received, precision=lax.Precision.HIGHEST))
    grad_z = jnp.einsum("g,gpr->pr", backward_row, received, precision=lax.Precision.HIGHEST)

    def ordered(own, other, other_first):
        return jnp.stack([jnp.where(other_first, other, own), jnp.where(other_first, own, other)])

    own_levels = jnp.concatenate([cross_x, grad_x[None]])
    near_levels = ordered(own_levels, swapped(own_levels, "core", 0), core_index == 1)
    z_part = jnp.concatenate([jnp.stack(cross_z), grad_z[None]])
    spread = jnp.broadcast_to(z_part[None], (8,) + z_part.shape)
    z_levels = lax.all_to_all(spread, ("x", "core"), 0, 0, tiled=True).reshape((4, 2) + z_part.shape)
    z_levels = z_levels.transpose(1, 2, 0, 3, 4).reshape(2, z_part.shape[0], head_size, head_size)
    device_grad = grad_first + near_levels[:, 2] + z_levels[:, -1]
    cross_list = [cross_first, near_levels[:, 0], near_levels[:, 1]] + [
        z_levels[:, level] for level in range(cross_levels - 3)
    ]
    level_table = bucket_table(per_dev, local_levels)
    local_buckets = jnp.einsum(
        "mji,ihpr->jmhpr", level_table, states, precision=lax.Precision.HIGHEST
    )
    cross_stack = jnp.stack(cross_list)
    cross_buckets = jnp.broadcast_to(cross_stack[None], (per_dev,) + cross_stack.shape)
    buckets = jnp.concatenate([local_buckets, cross_buckets], axis=1).astype(jnp.bfloat16)
    inter_out = jnp.einsum(
        "bthp,bmhpr->bmthr", query_rows, buckets, preferred_element_type=jnp.float32
    )
    output = output + jnp.sum(inter_w * inter_out, axis=1)
    inter_grad = jnp.einsum(
        "bmhpr,bthr->bmthp", buckets, cotan_rows, preferred_element_type=jnp.float32
    )
    grad_query = grad_query + jnp.sum(inter_w * inter_grad, axis=1)
    local_grad = jnp.einsum(
        "mji,jmhpr->ihpr",
        level_table,
        level_grads[:, :local_levels],
        precision=lax.Precision.HIGHEST,
    )
    state_grad = (local_grad + device_grad[None]).astype(jnp.bfloat16)
    grad_key = grad_key + jnp.einsum(
        "buhr,bhpr->buhp", value_rows, state_grad, preferred_element_type=jnp.float32
    )
    grad_value = grad_value + jnp.einsum(
        "buhp,bhpr->buhr", key_rows, state_grad, preferred_element_type=jnp.float32
    )

    def merge_rows(matrix):
        return matrix.reshape(tokens_dev, heads_local * head_size).astype(jnp.bfloat16)

    return (
        merge_rows(output),
        merge_rows(grad_query),
        merge_rows(grad_key),
        merge_rows(grad_value),
    )


def solution(mesh):
    seq_size, head_count = mesh.devices.shape
    split_mesh = Mesh(mesh.devices.reshape(seq_size // 8, 4, 2, head_count), ("z", "x", "core", "head"))
    seq_axes = ("z", "x", "core")
    placed = (
        P(seq_axes + ("head",), None),
        P(seq_axes + ("head",), None),
        P(seq_axes + ("head",), None),
        P(seq_axes + ("head",), None),
        P(None, "head", seq_axes),
    )
    return jax.shard_map(
        body,
        mesh=split_mesh,
        in_specs=placed,
        out_specs=(P(seq_axes, "head"),) * 4,
        check_vma=False,
    )
```

```python
import jax
import jax.numpy as jnp
import numpy as np
from jax import lax
from jax.sharding import Mesh, PartitionSpec as P

SPAN = 256


def swapped(value, axis, distance):
    mask = 2**distance
    pairs = [(source, source ^ mask) for source in range(lax.axis_size(axis))]
    return lax.ppermute(value, axis, pairs)


def bucket_table(per_dev, local_levels):
    level_table = np.zeros((local_levels, per_dev, per_dev), np.float32)
    for level in range(local_levels):
        for target in range(per_dev):
            begin_at = target >> (level + 1) << (level + 1)
            end_at = target >> level << level
            level_table[level, target, begin_at:end_at] = 1.0
    return jnp.asarray(level_table)


def z_tables(groups):
    levels = groups.bit_length() - 1
    choice = np.zeros((groups, groups), np.int32)
    forward_table = np.zeros((groups, levels, groups), np.float32)
    backward_table = np.zeros((groups, groups), np.float32)
    for own in range(groups):
        for other in range(groups):
            if other == own:
                continue
            level = (own ^ other).bit_length() - 1
            choice[own, other] = 1 if other > own else 2 + level
            if other < own:
                forward_table[own, level, other] = 1.0
            else:
                backward_table[own, other] = 1.0
    return jnp.asarray(choice), jnp.asarray(forward_table), jnp.asarray(backward_table)


def body(queries, key_vectors, value_vectors, grad_output, level_weights):
    stacked = jnp.stack([queries, key_vectors, value_vectors, grad_output], axis=1)
    exchanged = lax.all_to_all(stacked, "head", split_axis=2, concat_axis=0, tiled=True)
    query_in, key_in, value_in, cotan_in = (exchanged[:, index] for index in range(4))
    tokens_dev = query_in.shape[0]
    heads_local = level_weights.shape[1]
    head_size = query_in.shape[1] // heads_local
    levels_all = level_weights.shape[0]
    per_dev = tokens_dev // SPAN
    local_levels = per_dev.bit_length() - 1
    cross_levels = (lax.axis_size("z") * 8).bit_length() - 1

    def split_spans(matrix):
        return matrix.reshape(per_dev, SPAN, heads_local, head_size)

    query_rows = split_spans(query_in)
    key_rows = split_spans(key_in)
    value_rows = split_spans(value_in)
    cotan_rows = split_spans(cotan_in)
    gain_list = [(head_size * SPAN) ** (-0.5)] + [
        (head_size * 2**tree_level * SPAN) ** (-0.5) for tree_level in range(levels_all - 1)
    ]
    level_gains = jnp.array(gain_list, jnp.float32)
    weights = (level_weights.astype(jnp.float32) / 64.0 * level_gains[:, None, None]).reshape(
        levels_all, heads_local, per_dev, SPAN
    )
    intra_w = jnp.transpose(weights[0], (1, 0, 2))[:, :, :, None]
    inter_w = jnp.transpose(weights[1:], (2, 0, 3, 1))[..., None]
    position = jnp.arange(SPAN, dtype=jnp.int32)
    causal = position[:, None] >= position[None, :]
    scores = jnp.einsum("bthp,buhp->bhtu", query_rows, key_rows, preferred_element_type=jnp.float32)
    attention = jnp.where(causal, scores * intra_w, 0.0).astype(jnp.bfloat16)
    cotan_scores = jnp.einsum(
        "bthr,buhr->bhtu", cotan_rows, value_rows, preferred_element_type=jnp.float32
    )
    grad_scores = jnp.where(causal, cotan_scores * intra_w, 0.0).astype(jnp.bfloat16)
    output = jnp.einsum(
        "bhtu,buhr->bthr", attention, value_rows, preferred_element_type=jnp.float32
    )
    grad_query = jnp.einsum(
        "bhtu,buhp->bthp", grad_scores, key_rows, preferred_element_type=jnp.float32
    )
    grad_key = jnp.einsum(
        "bhtu,bthp->buhp", grad_scores, query_rows, preferred_element_type=jnp.float32
    )
    grad_value = jnp.einsum(
        "bhtu,bthr->buhr", attention, cotan_rows, preferred_element_type=jnp.float32
    )
    states = jnp.einsum("buhp,buhr->bhpr", key_rows, value_rows, preferred_element_type=jnp.float32)
    core_index = lax.axis_index("core")
    x_index = lax.axis_index("x")
    seq_index = (lax.axis_index("z") * 4 + x_index) * 2 + core_index
    upper_bits = (jnp.right_shift(seq_index, jnp.arange(cross_levels, dtype=jnp.int32)) % 2).astype(
        jnp.float32
    )
    weighted = (inter_w * cotan_rows[:, None]).astype(jnp.bfloat16)
    level_grads = jnp.einsum(
        "bthp,bmthr->bmhpr", query_rows, weighted, preferred_element_type=jnp.float32
    )
    running = jnp.sum(states, axis=0)
    pending = jnp.sum(level_grads[:, local_levels:], axis=0) * upper_bits[:, None, None, None]
    packet = jnp.concatenate([running[None], pending], axis=0)
    arrived = swapped(packet, "core", 0)
    cross_first = arrived[0] * upper_bits[0]
    grad_first = (1.0 - upper_bits[0]) * arrived[1]
    running = lax.dynamic_index_in_dim(running + arrived[0], core_index, 0, keepdims=False)
    pending = lax.dynamic_index_in_dim(pending[1:] + arrived[2:], core_index, 1, keepdims=False)
    quarter = head_size // 4
    x_choice, x_forward, x_backward = z_tables(lax.axis_size("x"))
    x_options = jnp.concatenate([jnp.zeros_like(running)[None], running[None], pending[:2]])
    near_chunks = jnp.take(x_options, lax.dynamic_index_in_dim(x_choice, x_index, 0, keepdims=False), axis=0)
    far_chunks = jnp.concatenate([running[None], pending[2:]]).reshape(-1, 4, quarter, head_size)
    x_send = jnp.concatenate([near_chunks.reshape(4, 4, quarter, head_size), far_chunks.transpose(1, 0, 2, 3)], axis=1)
    x_received = lax.all_to_all(x_send, "x", 0, 0, tiled=True)
    near_received = x_received[:, :4].reshape(4, head_size, head_size)
    cross_x = jnp.einsum(
        "jg,gpr->jpr",
        lax.dynamic_index_in_dim(x_forward, x_index, 0, keepdims=False),
        near_received,
        precision=lax.Precision.HIGHEST,
    )
    grad_x = jnp.einsum(
        "g,gpr->pr",
        lax.dynamic_index_in_dim(x_backward, x_index, 0, keepdims=False),
        near_received,
        precision=lax.Precision.HIGHEST,
    )
    far_received = jnp.sum(x_received[:, 4:], axis=0)
    running = far_received[0]
    pending = far_received[1:]
    z_count = lax.axis_size("z")
    z_index = lax.axis_index("z")
    choice, forward_table, backward_table = z_tables(z_count)
    options = jnp.concatenate([jnp.zeros_like(running)[None], running[None], pending])
    chunks = jnp.take(options, lax.dynamic_index_in_dim(choice, z_index, 0, keepdims=False), axis=0)
    received = lax.all_to_all(chunks, "z", 0, 0, tiled=True)
    forward_rows = lax.dynamic_index_in_dim(forward_table, z_index, 0, keepdims=False)
    backward_row = lax.dynamic_index_in_dim(backward_table, z_index, 0, keepdims=False)
    cross_z = list(jnp.einsum("jg,gpr->jpr", forward_rows, received, precision=lax.Precision.HIGHEST))
    grad_z = jnp.einsum("g,gpr->pr", backward_row, received, precision=lax.Precision.HIGHEST)

    def ordered(own, other, other_first):
        return jnp.stack([jnp.where(other_first, other, own), jnp.where(other_first, own, other)])

    own_levels = jnp.concatenate([cross_x, grad_x[None]])
    near_levels = ordered(own_levels, swapped(own_levels, "core", 0), core_index == 1)
    z_part = jnp.concatenate([jnp.stack(cross_z), grad_z[None]])
    spread = jnp.broadcast_to(z_part[None], (8,) + z_part.shape)
    z_levels = lax.all_to_all(spread, ("x", "core"), 0, 0, tiled=True).reshape((4, 2) + z_part.shape)
    z_levels = z_levels.transpose(1, 2, 0, 3, 4).reshape(2, z_part.shape[0], head_size, head_size)
    device_grad = grad_first + near_levels[:, 2] + z_levels[:, -1]
    cross_list = [cross_first, near_levels[:, 0], near_levels[:, 1]]
    level_table = bucket_table(per_dev, local_levels)
    local_buckets = jnp.einsum(
        "mji,ihpr->jmhpr", level_table, states, precision=lax.Precision.HIGHEST
    )
    early_cross = jnp.stack(cross_list)
    late_cross = z_levels[:, : cross_levels - 3].transpose(1, 0, 2, 3)
    early_levels = local_levels + early_cross.shape[0]
    bucket_groups = (
        (jnp.concatenate([local_buckets, jnp.broadcast_to(early_cross[None], (per_dev,) + early_cross.shape)], axis=1), slice(0, early_levels)),
        (jnp.broadcast_to(late_cross[None], (per_dev,) + late_cross.shape), slice(early_levels, None)),
    )
    for group, level_slice in bucket_groups:
        buckets = group.astype(jnp.bfloat16)
        group_w = inter_w[:, level_slice]
        inter_out = jnp.einsum(
            "bthp,bmhpr->bmthr", query_rows, buckets, preferred_element_type=jnp.float32
        )
        output = output + jnp.sum(group_w * inter_out, axis=1)
        inter_grad = jnp.einsum(
            "bmhpr,bthr->bmthp", buckets, cotan_rows, preferred_element_type=jnp.float32
        )
        grad_query = grad_query + jnp.sum(group_w * inter_grad, axis=1)
    local_grad = jnp.einsum(
        "mji,jmhpr->ihpr",
        level_table,
        level_grads[:, :local_levels],
        precision=lax.Precision.HIGHEST,
    )
    state_grad = (local_grad + device_grad[None]).astype(jnp.bfloat16)
    grad_key = grad_key + jnp.einsum(
        "buhr,bhpr->buhp", value_rows, state_grad, preferred_element_type=jnp.float32
    )
    grad_value = grad_value + jnp.einsum(
        "buhp,bhpr->buhr", key_rows, state_grad, preferred_element_type=jnp.float32
    )

    def merge_rows(matrix):
        return matrix.reshape(tokens_dev, heads_local * head_size).astype(jnp.bfloat16)

    return (
        merge_rows(output),
        merge_rows(grad_query),
        merge_rows(grad_key),
        merge_rows(grad_value),
    )


def solution(mesh):
    seq_size, head_count = mesh.devices.shape
    split_mesh = Mesh(mesh.devices.reshape(seq_size // 8, 4, 2, head_count), ("z", "x", "core", "head"))
    seq_axes = ("z", "x", "core")
    placed = (
        P(seq_axes + ("head",), None),
        P(seq_axes + ("head",), None),
        P(seq_axes + ("head",), None),
        P(seq_axes + ("head",), None),
        P(None, "head", seq_axes),
    )
    return jax.shard_map(
        body,
        mesh=split_mesh,
        in_specs=placed,
        out_specs=(P(seq_axes, "head"),) * 4,
        check_vma=False,
    )
```

```python
import jax
import jax.numpy as jnp
import numpy as np
from jax import lax
from jax.sharding import Mesh, PartitionSpec as P

SPAN = 256


def swapped(value, axis, distance):
    mask = 2**distance
    pairs = [(source, source ^ mask) for source in range(lax.axis_size(axis))]
    return lax.ppermute(value, axis, pairs)


def bucket_table(per_dev, local_levels):
    level_table = np.zeros((local_levels, per_dev, per_dev), np.float32)
    for level in range(local_levels):
        for target in range(per_dev):
            begin_at = target >> (level + 1) << (level + 1)
            end_at = target >> level << level
            level_table[level, target, begin_at:end_at] = 1.0
    return jnp.asarray(level_table)


def z_tables(groups):
    levels = groups.bit_length() - 1
    choice = np.zeros((groups, groups), np.int32)
    forward_table = np.zeros((groups, levels, groups), np.float32)
    backward_table = np.zeros((groups, groups), np.float32)
    for own in range(groups):
        for other in range(groups):
            if other == own:
                continue
            level = (own ^ other).bit_length() - 1
            choice[own, other] = 1 if other > own else 2 + level
            if other < own:
                forward_table[own, level, other] = 1.0
            else:
                backward_table[own, other] = 1.0
    return jnp.asarray(choice), jnp.asarray(forward_table), jnp.asarray(backward_table)


def body(queries, key_vectors, value_vectors, grad_output, level_weights):
    stacked = jnp.stack([queries, key_vectors, value_vectors, grad_output], axis=1)
    exchanged = lax.all_to_all(stacked, "head", split_axis=2, concat_axis=0, tiled=True)
    query_in, key_in, value_in, cotan_in = (exchanged[:, index] for index in range(4))
    tokens_dev = query_in.shape[0]
    heads_local = level_weights.shape[1]
    head_size = query_in.shape[1] // heads_local
    levels_all = level_weights.shape[0]
    per_dev = tokens_dev // SPAN
    local_levels = per_dev.bit_length() - 1
    cross_levels = (lax.axis_size("z") * 8).bit_length() - 1

    def split_spans(matrix):
        return matrix.reshape(per_dev, SPAN, heads_local, head_size)

    query_rows = split_spans(query_in)
    key_rows = split_spans(key_in)
    value_rows = split_spans(value_in)
    cotan_rows = split_spans(cotan_in)
    gain_list = [(head_size * SPAN) ** (-0.5)] + [
        (head_size * 2**tree_level * SPAN) ** (-0.5) for tree_level in range(levels_all - 1)
    ]
    level_gains = jnp.array(gain_list, jnp.float32)
    weights = (level_weights.astype(jnp.float32) / 64.0 * level_gains[:, None, None]).reshape(
        levels_all, heads_local, per_dev, SPAN
    )
    intra_w = jnp.transpose(weights[0], (1, 0, 2))[:, :, :, None]
    inter_w = jnp.transpose(weights[1:], (2, 0, 3, 1))[..., None]
    position = jnp.arange(SPAN, dtype=jnp.int32)
    causal = position[:, None] >= position[None, :]
    states = jnp.einsum("buhp,buhr->bhpr", key_rows, value_rows, preferred_element_type=jnp.float32)
    core_index = lax.axis_index("core")
    x_index = lax.axis_index("x")
    seq_index = (lax.axis_index("z") * 4 + x_index) * 2 + core_index
    upper_bits = (jnp.right_shift(seq_index, jnp.arange(cross_levels, dtype=jnp.int32)) % 2).astype(
        jnp.float32
    )
    weighted = (inter_w * cotan_rows[:, None]).astype(jnp.bfloat16)
    level_grads = jnp.einsum(
        "bthp,bmthr->bmhpr", query_rows, weighted, preferred_element_type=jnp.float32
    )
    running = jnp.sum(states, axis=0)
    pending = jnp.sum(level_grads[:, local_levels:], axis=0) * upper_bits[:, None, None, None]
    packet = jnp.concatenate([running[None], pending], axis=0)
    arrived = swapped(packet, "core", 0)
    cross_first = arrived[0] * upper_bits[0]
    grad_first = (1.0 - upper_bits[0]) * arrived[1]
    running = lax.dynamic_index_in_dim(running + arrived[0], core_index, 0, keepdims=False)
    pending = lax.dynamic_index_in_dim(pending[1:] + arrived[2:], core_index, 1, keepdims=False)
    quarter = head_size // 4
    x_choice, x_forward, x_backward = z_tables(lax.axis_size("x"))
    x_options = jnp.concatenate([jnp.zeros_like(running)[None], running[None], pending[:2]])
    near_chunks = jnp.take(x_options, lax.dynamic_index_in_dim(x_choice, x_index, 0, keepdims=False), axis=0)
    far_chunks = jnp.concatenate([running[None], pending[2:]]).reshape(-1, 4, quarter, head_size)
    x_send = jnp.concatenate([near_chunks.reshape(4, 4, quarter, head_size), far_chunks.transpose(1, 0, 2, 3)], axis=1)
    x_received = lax.all_to_all(x_send, "x", 0, 0, tiled=True)
    near_received = x_received[:, :4].reshape(4, head_size, head_size)
    cross_x = jnp.einsum(
        "jg,gpr->jpr",
        lax.dynamic_index_in_dim(x_forward, x_index, 0, keepdims=False),
        near_received,
        precision=lax.Precision.HIGHEST,
    )
    grad_x = jnp.einsum(
        "g,gpr->pr",
        lax.dynamic_index_in_dim(x_backward, x_index, 0, keepdims=False),
        near_received,
        precision=lax.Precision.HIGHEST,
    )
    far_received = jnp.sum(x_received[:, 4:], axis=0)
    running = far_received[0]
    pending = far_received[1:]
    z_count = lax.axis_size("z")
    z_index = lax.axis_index("z")
    choice, forward_table, backward_table = z_tables(z_count)
    options = jnp.concatenate([jnp.zeros_like(running)[None], running[None], pending])
    chunks = jnp.take(options, lax.dynamic_index_in_dim(choice, z_index, 0, keepdims=False), axis=0)
    received = lax.all_to_all(chunks, "z", 0, 0, tiled=True)
    late_query, late_key, late_value, late_cotan, _ = lax.optimization_barrier(
        (query_rows, key_rows, value_rows, cotan_rows, received)
    )
    scores = jnp.einsum("bthp,buhp->bhtu", late_query, late_key, preferred_element_type=jnp.float32)
    attention = jnp.where(causal, scores * intra_w, 0.0).astype(jnp.bfloat16)
    cotan_scores = jnp.einsum(
        "bthr,buhr->bhtu", late_cotan, late_value, preferred_element_type=jnp.float32
    )
    grad_scores = jnp.where(causal, cotan_scores * intra_w, 0.0).astype(jnp.bfloat16)
    output = jnp.einsum(
        "bhtu,buhr->bthr", attention, late_value, preferred_element_type=jnp.float32
    )
    grad_query = jnp.einsum(
        "bhtu,buhp->bthp", grad_scores, late_key, preferred_element_type=jnp.float32
    )
    grad_key = jnp.einsum(
        "bhtu,bthp->buhp", grad_scores, late_query, preferred_element_type=jnp.float32
    )
    grad_value = jnp.einsum(
        "bhtu,bthr->buhr", attention, late_cotan, preferred_element_type=jnp.float32
    )
    forward_rows = lax.dynamic_index_in_dim(forward_table, z_index, 0, keepdims=False)
    backward_row = lax.dynamic_index_in_dim(backward_table, z_index, 0, keepdims=False)
    cross_z = list(jnp.einsum("jg,gpr->jpr", forward_rows, received, precision=lax.Precision.HIGHEST))
    grad_z = jnp.einsum("g,gpr->pr", backward_row, received, precision=lax.Precision.HIGHEST)

    def ordered(own, other, other_first):
        return jnp.stack([jnp.where(other_first, other, own), jnp.where(other_first, own, other)])

    own_levels = jnp.concatenate([cross_x, grad_x[None]])
    near_levels = ordered(own_levels, swapped(own_levels, "core", 0), core_index == 1)
    z_part = jnp.concatenate([jnp.stack(cross_z), grad_z[None]])
    spread = jnp.broadcast_to(z_part[None], (8,) + z_part.shape)
    z_levels = lax.all_to_all(spread, ("x", "core"), 0, 0, tiled=True).reshape((4, 2) + z_part.shape)
    z_levels = z_levels.transpose(1, 2, 0, 3, 4).reshape(2, z_part.shape[0], head_size, head_size)
    device_grad = grad_first + near_levels[:, 2] + z_levels[:, -1]
    cross_list = [cross_first, near_levels[:, 0], near_levels[:, 1]]
    level_table = bucket_table(per_dev, local_levels)
    local_buckets = jnp.einsum(
        "mji,ihpr->jmhpr", level_table, states, precision=lax.Precision.HIGHEST
    )
    early_cross = jnp.stack(cross_list)
    late_cross = z_levels[:, : cross_levels - 3].transpose(1, 0, 2, 3)
    early_levels = local_levels + early_cross.shape[0]
    bucket_groups = (
        (jnp.concatenate([local_buckets, jnp.broadcast_to(early_cross[None], (per_dev,) + early_cross.shape)], axis=1), slice(0, early_levels)),
        (jnp.broadcast_to(late_cross[None], (per_dev,) + late_cross.shape), slice(early_levels, None)),
    )
    for group, level_slice in bucket_groups:
        buckets = group.astype(jnp.bfloat16)
        group_w = inter_w[:, level_slice]
        inter_out = jnp.einsum(
            "bthp,bmhpr->bmthr", query_rows, buckets, preferred_element_type=jnp.float32
        )
        output = output + jnp.sum(group_w * inter_out, axis=1)
        inter_grad = jnp.einsum(
            "bmhpr,bthr->bmthp", buckets, cotan_rows, preferred_element_type=jnp.float32
        )
        grad_query = grad_query + jnp.sum(group_w * inter_grad, axis=1)
    local_grad = jnp.einsum(
        "mji,jmhpr->ihpr",
        level_table,
        level_grads[:, :local_levels],
        precision=lax.Precision.HIGHEST,
    )
    state_grad = (local_grad + device_grad[None]).astype(jnp.bfloat16)
    grad_key = grad_key + jnp.einsum(
        "buhr,bhpr->buhp", value_rows, state_grad, preferred_element_type=jnp.float32
    )
    grad_value = grad_value + jnp.einsum(
        "buhp,bhpr->buhr", key_rows, state_grad, preferred_element_type=jnp.float32
    )

    def merge_rows(matrix):
        return matrix.reshape(tokens_dev, heads_local * head_size).astype(jnp.bfloat16)

    return (
        merge_rows(output),
        merge_rows(grad_query),
        merge_rows(grad_key),
        merge_rows(grad_value),
    )


def solution(mesh):
    seq_size, head_count = mesh.devices.shape
    split_mesh = Mesh(mesh.devices.reshape(seq_size // 8, 4, 2, head_count), ("z", "x", "core", "head"))
    seq_axes = ("z", "x", "core")
    placed = (
        P(seq_axes + ("head",), None),
        P(seq_axes + ("head",), None),
        P(seq_axes + ("head",), None),
        P(seq_axes + ("head",), None),
        P(None, "head", seq_axes),
    )
    return jax.shard_map(
        body,
        mesh=split_mesh,
        in_specs=placed,
        out_specs=(P(seq_axes, "head"),) * 4,
        check_vma=False,
    )
```

```python
import jax
import jax.numpy as jnp
import numpy as np
from jax import lax
from jax.sharding import Mesh, PartitionSpec as P

SPAN = 256


def swapped(value, axis, distance):
    mask = 2**distance
    pairs = [(source, source ^ mask) for source in range(lax.axis_size(axis))]
    return lax.ppermute(value, axis, pairs)


def bucket_table(per_dev, local_levels):
    level_table = np.zeros((local_levels, per_dev, per_dev), np.float32)
    for level in range(local_levels):
        for target in range(per_dev):
            begin_at = target >> (level + 1) << (level + 1)
            end_at = target >> level << level
            level_table[level, target, begin_at:end_at] = 1.0
    return jnp.asarray(level_table)


def z_tables(groups):
    levels = groups.bit_length() - 1
    choice = np.zeros((groups, groups), np.int32)
    forward_table = np.zeros((groups, levels, groups), np.float32)
    backward_table = np.zeros((groups, groups), np.float32)
    for own in range(groups):
        for other in range(groups):
            if other == own:
                continue
            level = (own ^ other).bit_length() - 1
            choice[own, other] = 1 if other > own else 2 + level
            if other < own:
                forward_table[own, level, other] = 1.0
            else:
                backward_table[own, other] = 1.0
    return jnp.asarray(choice), jnp.asarray(forward_table), jnp.asarray(backward_table)


def body(queries, key_vectors, value_vectors, grad_output, level_weights):
    head_groups = lax.axis_size("head")
    stacked = jnp.stack(
        [matrix.reshape(matrix.shape[0], head_groups, -1) for matrix in (queries, key_vectors, value_vectors, grad_output)],
        axis=0,
    )
    exchanged = lax.all_to_all(stacked, "head", split_axis=2, concat_axis=1, tiled=True)
    query_in, key_in, value_in, cotan_in = (exchanged[index].reshape(exchanged.shape[1], -1) for index in range(4))
    tokens_dev = query_in.shape[0]
    heads_local = level_weights.shape[1]
    head_size = query_in.shape[1] // heads_local
    levels_all = level_weights.shape[0]
    per_dev = tokens_dev // SPAN
    local_levels = per_dev.bit_length() - 1
    cross_levels = (lax.axis_size("z") * 8).bit_length() - 1

    def split_spans(matrix):
        return matrix.reshape(per_dev, SPAN, heads_local, head_size)

    query_rows = split_spans(query_in)
    key_rows = split_spans(key_in)
    value_rows = split_spans(value_in)
    cotan_rows = split_spans(cotan_in)
    gain_list = [(head_size * SPAN) ** (-0.5)] + [
        (head_size * 2**tree_level * SPAN) ** (-0.5) for tree_level in range(levels_all - 1)
    ]
    level_gains = jnp.array(gain_list, jnp.float32)
    weights = (level_weights.astype(jnp.float32) / 64.0 * level_gains[:, None, None]).reshape(
        levels_all, heads_local, per_dev, SPAN
    )
    intra_w = jnp.transpose(weights[0], (1, 0, 2))[:, :, :, None]
    inter_w = jnp.transpose(weights[1:], (2, 0, 3, 1))[..., None]
    position = jnp.arange(SPAN, dtype=jnp.int32)
    causal = position[:, None] >= position[None, :]
    states = jnp.einsum("buhp,buhr->bhpr", key_rows, value_rows, preferred_element_type=jnp.float32)
    core_index = lax.axis_index("core")
    x_index = lax.axis_index("x")
    seq_index = (lax.axis_index("z") * 4 + x_index) * 2 + core_index
    upper_bits = (jnp.right_shift(seq_index, jnp.arange(cross_levels, dtype=jnp.int32)) % 2).astype(
        jnp.float32
    )
    weighted = (inter_w * cotan_rows[:, None]).astype(jnp.bfloat16)
    level_grads = jnp.einsum(
        "bthp,bmthr->bmhpr", query_rows, weighted, preferred_element_type=jnp.float32
    )
    running = jnp.sum(states, axis=0)
    pending = jnp.sum(level_grads[:, local_levels:], axis=0) * upper_bits[:, None, None, None]
    packet = jnp.concatenate([running[None], pending], axis=0)
    arrived = swapped(packet, "core", 0)
    cross_first = arrived[0] * upper_bits[0]
    grad_first = (1.0 - upper_bits[0]) * arrived[1]
    running = lax.dynamic_index_in_dim(running + arrived[0], core_index, 0, keepdims=False)
    pending = lax.dynamic_index_in_dim(pending[1:] + arrived[2:], core_index, 1, keepdims=False)
    quarter = head_size // 4
    x_choice, x_forward, x_backward = z_tables(lax.axis_size("x"))
    x_options = jnp.concatenate([jnp.zeros_like(running)[None], running[None], pending[:2]])
    near_chunks = jnp.take(x_options, lax.dynamic_index_in_dim(x_choice, x_index, 0, keepdims=False), axis=0)
    far_chunks = jnp.concatenate([running[None], pending[2:]]).reshape(-1, 4, quarter, head_size)
    x_send = jnp.concatenate([near_chunks.reshape(4, 4, quarter, head_size), far_chunks.transpose(1, 0, 2, 3)], axis=1)
    x_received = lax.all_to_all(x_send, "x", 0, 0, tiled=True)
    near_received = x_received[:, :4].reshape(4, head_size, head_size)
    cross_x = jnp.einsum(
        "jg,gpr->jpr",
        lax.dynamic_index_in_dim(x_forward, x_index, 0, keepdims=False),
        near_received,
        precision=lax.Precision.HIGHEST,
    )
    grad_x = jnp.einsum(
        "g,gpr->pr",
        lax.dynamic_index_in_dim(x_backward, x_index, 0, keepdims=False),
        near_received,
        precision=lax.Precision.HIGHEST,
    )
    far_received = jnp.sum(x_received[:, 4:], axis=0)
    running = far_received[0]
    pending = far_received[1:]
    z_count = lax.axis_size("z")
    z_index = lax.axis_index("z")
    choice, forward_table, backward_table = z_tables(z_count)
    options = jnp.concatenate([jnp.zeros_like(running)[None], running[None], pending])
    chunks = jnp.take(options, lax.dynamic_index_in_dim(choice, z_index, 0, keepdims=False), axis=0)
    received = lax.all_to_all(chunks, "z", 0, 0, tiled=True)
    late_query, late_key, late_value, late_cotan, _ = lax.optimization_barrier(
        (query_rows, key_rows, value_rows, cotan_rows, received)
    )
    scores = jnp.einsum("bthp,buhp->bhtu", late_query, late_key, preferred_element_type=jnp.float32)
    attention = jnp.where(causal, scores * intra_w, 0.0).astype(jnp.bfloat16)
    cotan_scores = jnp.einsum(
        "bthr,buhr->bhtu", late_cotan, late_value, preferred_element_type=jnp.float32
    )
    grad_scores = jnp.where(causal, cotan_scores * intra_w, 0.0).astype(jnp.bfloat16)
    output = jnp.einsum(
        "bhtu,buhr->bthr", attention, late_value, preferred_element_type=jnp.float32
    )
    grad_query = jnp.einsum(
        "bhtu,buhp->bthp", grad_scores, late_key, preferred_element_type=jnp.float32
    )
    grad_key = jnp.einsum(
        "bhtu,bthp->buhp", grad_scores, late_query, preferred_element_type=jnp.float32
    )
    grad_value = jnp.einsum(
        "bhtu,bthr->buhr", attention, late_cotan, preferred_element_type=jnp.float32
    )
    forward_rows = lax.dynamic_index_in_dim(forward_table, z_index, 0, keepdims=False)
    backward_row = lax.dynamic_index_in_dim(backward_table, z_index, 0, keepdims=False)
    cross_z = list(jnp.einsum("jg,gpr->jpr", forward_rows, received, precision=lax.Precision.HIGHEST))
    grad_z = jnp.einsum("g,gpr->pr", backward_row, received, precision=lax.Precision.HIGHEST)

    def ordered(own, other, other_first):
        return jnp.stack([jnp.where(other_first, other, own), jnp.where(other_first, own, other)])

    own_levels = jnp.concatenate([cross_x, grad_x[None]])
    near_levels = ordered(own_levels, swapped(own_levels, "core", 0), core_index == 1)
    z_part = jnp.concatenate([jnp.stack(cross_z), grad_z[None]])
    spread = jnp.broadcast_to(z_part[None], (8,) + z_part.shape)
    z_levels = lax.all_to_all(spread, ("x", "core"), 0, 0, tiled=True).reshape((4, 2) + z_part.shape)
    z_levels = z_levels.transpose(1, 2, 0, 3, 4).reshape(2, z_part.shape[0], head_size, head_size)
    device_grad = grad_first + near_levels[:, 2] + z_levels[:, -1]
    cross_list = [cross_first, near_levels[:, 0], near_levels[:, 1]]
    level_table = bucket_table(per_dev, local_levels)
    local_buckets = jnp.einsum(
        "mji,ihpr->jmhpr", level_table, states, precision=lax.Precision.HIGHEST
    )
    early_cross = jnp.stack(cross_list)
    late_cross = z_levels[:, : cross_levels - 3].transpose(1, 0, 2, 3)
    early_levels = local_levels + early_cross.shape[0]
    bucket_groups = (
        (jnp.concatenate([local_buckets, jnp.broadcast_to(early_cross[None], (per_dev,) + early_cross.shape)], axis=1), slice(0, early_levels)),
        (jnp.broadcast_to(late_cross[None], (per_dev,) + late_cross.shape), slice(early_levels, None)),
    )
    for group, level_slice in bucket_groups:
        buckets = group.astype(jnp.bfloat16)
        group_w = inter_w[:, level_slice]
        inter_out = jnp.einsum(
            "bthp,bmhpr->bmthr", query_rows, buckets, preferred_element_type=jnp.float32
        )
        output = output + jnp.sum(group_w * inter_out, axis=1)
        inter_grad = jnp.einsum(
            "bmhpr,bthr->bmthp", buckets, cotan_rows, preferred_element_type=jnp.float32
        )
        grad_query = grad_query + jnp.sum(group_w * inter_grad, axis=1)
    local_grad = jnp.einsum(
        "mji,jmhpr->ihpr",
        level_table,
        level_grads[:, :local_levels],
        precision=lax.Precision.HIGHEST,
    )
    state_grad = (local_grad + device_grad[None]).astype(jnp.bfloat16)
    grad_key = grad_key + jnp.einsum(
        "buhr,bhpr->buhp", value_rows, state_grad, preferred_element_type=jnp.float32
    )
    grad_value = grad_value + jnp.einsum(
        "buhp,bhpr->buhr", key_rows, state_grad, preferred_element_type=jnp.float32
    )

    def merge_rows(matrix):
        return matrix.reshape(tokens_dev, heads_local * head_size).astype(jnp.bfloat16)

    return (
        merge_rows(output),
        merge_rows(grad_query),
        merge_rows(grad_key),
        merge_rows(grad_value),
    )


def solution(mesh):
    seq_size, head_count = mesh.devices.shape
    split_mesh = Mesh(mesh.devices.reshape(seq_size // 8, 4, 2, head_count), ("z", "x", "core", "head"))
    seq_axes = ("z", "x", "core")
    placed = (
        P(seq_axes + ("head",), None),
        P(seq_axes + ("head",), None),
        P(seq_axes + ("head",), None),
        P(seq_axes + ("head",), None),
        P(None, "head", seq_axes),
    )
    return jax.shard_map(
        body,
        mesh=split_mesh,
        in_specs=placed,
        out_specs=(P(seq_axes, "head"),) * 4,
        check_vma=False,
    )
```

```python
import jax
import jax.numpy as jnp
import numpy as np
from jax import lax
from jax.sharding import Mesh, PartitionSpec as P

SPAN = 256


def swapped(value, axis, distance):
    mask = 2**distance
    pairs = [(source, source ^ mask) for source in range(lax.axis_size(axis))]
    return lax.ppermute(value, axis, pairs)


def bucket_table(per_dev, local_levels):
    level_table = np.zeros((local_levels, per_dev, per_dev), np.float32)
    for level in range(local_levels):
        for target in range(per_dev):
            begin_at = target >> (level + 1) << (level + 1)
            end_at = target >> level << level
            level_table[level, target, begin_at:end_at] = 1.0
    return jnp.asarray(level_table)


def z_tables(groups):
    levels = groups.bit_length() - 1
    choice = np.zeros((groups, groups), np.int32)
    forward_table = np.zeros((groups, levels, groups), np.float32)
    backward_table = np.zeros((groups, groups), np.float32)
    for own in range(groups):
        for other in range(groups):
            if other == own:
                continue
            level = (own ^ other).bit_length() - 1
            choice[own, other] = 1 if other > own else 2 + level
            if other < own:
                forward_table[own, level, other] = 1.0
            else:
                backward_table[own, other] = 1.0
    return jnp.asarray(choice), jnp.asarray(forward_table), jnp.asarray(backward_table)


def body(queries, key_vectors, value_vectors, grad_output, level_weights):
    head_groups = lax.axis_size("head")
    stacked = jnp.stack(
        [matrix.reshape(matrix.shape[0], head_groups, -1) for matrix in (queries, key_vectors, value_vectors, grad_output)],
        axis=0,
    )
    exchanged = lax.all_to_all(stacked, "head", split_axis=2, concat_axis=1, tiled=True)
    query_in, key_in, value_in, cotan_in = (exchanged[index].reshape(exchanged.shape[1], -1) for index in range(4))
    tokens_dev = query_in.shape[0]
    heads_local = level_weights.shape[1]
    head_size = query_in.shape[1] // heads_local
    levels_all = level_weights.shape[0]
    per_dev = tokens_dev // SPAN
    local_levels = per_dev.bit_length() - 1
    cross_levels = (lax.axis_size("z") * 8).bit_length() - 1

    def split_spans(matrix):
        return matrix.reshape(per_dev, SPAN, heads_local, head_size)

    query_rows = split_spans(query_in)
    key_rows = split_spans(key_in)
    value_rows = split_spans(value_in)
    cotan_rows = split_spans(cotan_in)
    gain_list = [(head_size * SPAN) ** (-0.5)] + [
        (head_size * 2**tree_level * SPAN) ** (-0.5) for tree_level in range(levels_all - 1)
    ]
    level_gains = jnp.array(gain_list, jnp.float32)
    weights = (level_weights.astype(jnp.float32) / 64.0 * level_gains[:, None, None]).reshape(
        levels_all, heads_local, per_dev, SPAN
    )
    intra_w = jnp.transpose(weights[0], (1, 0, 2))[:, :, :, None]
    inter_w = jnp.transpose(weights[1:], (2, 0, 3, 1))[..., None]
    position = jnp.arange(SPAN, dtype=jnp.int32)
    causal = position[:, None] >= position[None, :]
    states = jnp.einsum("buhp,buhr->bhpr", key_rows, value_rows, preferred_element_type=jnp.float32)
    core_index = lax.axis_index("core")
    x_index = lax.axis_index("x")
    seq_index = (lax.axis_index("z") * 4 + x_index) * 2 + core_index
    upper_bits = (jnp.right_shift(seq_index, jnp.arange(cross_levels, dtype=jnp.int32)) % 2).astype(
        jnp.float32
    )
    weighted = (inter_w * cotan_rows[:, None]).astype(jnp.bfloat16)
    level_grads = jnp.einsum(
        "bthp,bmthr->bmhpr", query_rows, weighted, preferred_element_type=jnp.float32
    )
    running = jnp.sum(states, axis=0)
    pending = jnp.sum(level_grads[:, local_levels:], axis=0) * upper_bits[:, None, None, None]
    packet = jnp.concatenate([running[None], pending], axis=0)
    arrived = swapped(packet, "core", 0)
    cross_first = arrived[0] * upper_bits[0]
    grad_first = (1.0 - upper_bits[0]) * arrived[1]
    running = lax.dynamic_index_in_dim(running + arrived[0], core_index, 0, keepdims=False)
    pending = lax.dynamic_index_in_dim(pending[1:] + arrived[2:], core_index, 1, keepdims=False)
    quarter = head_size // 4
    x_choice, x_forward, x_backward = z_tables(lax.axis_size("x"))
    x_options = jnp.concatenate([jnp.zeros_like(running)[None], running[None], pending[:2]])
    near_chunks = jnp.take(x_options, lax.dynamic_index_in_dim(x_choice, x_index, 0, keepdims=False), axis=0)
    far_chunks = jnp.concatenate([running[None], pending[2:]]).reshape(-1, 4, quarter, head_size)
    x_send = jnp.concatenate([near_chunks.reshape(4, 4, quarter, head_size), far_chunks.transpose(1, 0, 2, 3)], axis=1)
    x_received = lax.all_to_all(x_send, "x", 0, 0, tiled=True)
    near_received = x_received[:, :4].reshape(4, head_size, head_size)
    cross_x = jnp.einsum(
        "jg,gpr->jpr",
        lax.dynamic_index_in_dim(x_forward, x_index, 0, keepdims=False),
        near_received,
        precision=lax.Precision.HIGHEST,
    )
    grad_x = jnp.einsum(
        "g,gpr->pr",
        lax.dynamic_index_in_dim(x_backward, x_index, 0, keepdims=False),
        near_received,
        precision=lax.Precision.HIGHEST,
    )
    far_received = jnp.sum(x_received[:, 4:], axis=0)
    running = far_received[0]
    pending = far_received[1:]
    z_count = lax.axis_size("z")
    z_index = lax.axis_index("z")
    choice, forward_table, backward_table = z_tables(z_count)
    options = jnp.concatenate([jnp.zeros_like(running)[None], running[None], pending])
    chunks = jnp.take(options, lax.dynamic_index_in_dim(choice, z_index, 0, keepdims=False), axis=0)
    received = lax.all_to_all(chunks, "z", 0, 0, tiled=True)
    late_query, late_key, late_value, late_cotan, _ = lax.optimization_barrier(
        (query_rows, key_rows, value_rows, cotan_rows, chunks)
    )
    scores = jnp.einsum("bthp,buhp->bhtu", late_query, late_key, preferred_element_type=jnp.float32)
    attention = jnp.where(causal, scores * intra_w, 0.0).astype(jnp.bfloat16)
    cotan_scores = jnp.einsum(
        "bthr,buhr->bhtu", late_cotan, late_value, preferred_element_type=jnp.float32
    )
    grad_scores = jnp.where(causal, cotan_scores * intra_w, 0.0).astype(jnp.bfloat16)
    output = jnp.einsum(
        "bhtu,buhr->bthr", attention, late_value, preferred_element_type=jnp.float32
    )
    grad_query = jnp.einsum(
        "bhtu,buhp->bthp", grad_scores, late_key, preferred_element_type=jnp.float32
    )
    grad_key = jnp.einsum(
        "bhtu,bthp->buhp", grad_scores, late_query, preferred_element_type=jnp.float32
    )
    grad_value = jnp.einsum(
        "bhtu,bthr->buhr", attention, late_cotan, preferred_element_type=jnp.float32
    )
    forward_rows = lax.dynamic_index_in_dim(forward_table, z_index, 0, keepdims=False)
    backward_row = lax.dynamic_index_in_dim(backward_table, z_index, 0, keepdims=False)
    cross_z = list(jnp.einsum("jg,gpr->jpr", forward_rows, received, precision=lax.Precision.HIGHEST))
    grad_z = jnp.einsum("g,gpr->pr", backward_row, received, precision=lax.Precision.HIGHEST)

    def ordered(own, other, other_first):
        return jnp.stack([jnp.where(other_first, other, own), jnp.where(other_first, own, other)])

    own_levels = jnp.concatenate([cross_x, grad_x[None]])
    near_levels = ordered(own_levels, swapped(own_levels, "core", 0), core_index == 1)
    z_part = jnp.concatenate([jnp.stack(cross_z), grad_z[None]])
    spread = jnp.broadcast_to(z_part[None], (8,) + z_part.shape)
    z_levels = lax.all_to_all(spread, ("x", "core"), 0, 0, tiled=True).reshape((4, 2) + z_part.shape)
    z_levels = z_levels.transpose(1, 2, 0, 3, 4).reshape(2, z_part.shape[0], head_size, head_size)
    device_grad = grad_first + near_levels[:, 2] + z_levels[:, -1]
    cross_list = [cross_first, near_levels[:, 0], near_levels[:, 1]]
    level_table = bucket_table(per_dev, local_levels)
    local_buckets = jnp.einsum(
        "mji,ihpr->jmhpr", level_table, states, precision=lax.Precision.HIGHEST
    )
    early_cross = jnp.stack(cross_list)
    late_cross = z_levels[:, : cross_levels - 3].transpose(1, 0, 2, 3)
    early_levels = local_levels + early_cross.shape[0]
    bucket_groups = (
        (jnp.concatenate([local_buckets, jnp.broadcast_to(early_cross[None], (per_dev,) + early_cross.shape)], axis=1), slice(0, early_levels)),
        (jnp.broadcast_to(late_cross[None], (per_dev,) + late_cross.shape), slice(early_levels, None)),
    )
    for group, level_slice in bucket_groups:
        buckets = group.astype(jnp.bfloat16)
        group_w = inter_w[:, level_slice]
        inter_out = jnp.einsum(
            "bthp,bmhpr->bmthr", query_rows, buckets, preferred_element_type=jnp.float32
        )
        output = output + jnp.sum(group_w * inter_out, axis=1)
        inter_grad = jnp.einsum(
            "bmhpr,bthr->bmthp", buckets, cotan_rows, preferred_element_type=jnp.float32
        )
        grad_query = grad_query + jnp.sum(group_w * inter_grad, axis=1)
    local_grad = jnp.einsum(
        "mji,jmhpr->ihpr",
        level_table,
        level_grads[:, :local_levels],
        precision=lax.Precision.HIGHEST,
    )
    state_grad = (local_grad + device_grad[None]).astype(jnp.bfloat16)
    grad_key = grad_key + jnp.einsum(
        "buhr,bhpr->buhp", value_rows, state_grad, preferred_element_type=jnp.float32
    )
    grad_value = grad_value + jnp.einsum(
        "buhp,bhpr->buhr", key_rows, state_grad, preferred_element_type=jnp.float32
    )

    def merge_rows(matrix):
        return matrix.reshape(tokens_dev, heads_local * head_size).astype(jnp.bfloat16)

    return (
        merge_rows(output),
        merge_rows(grad_query),
        merge_rows(grad_key),
        merge_rows(grad_value),
    )


def solution(mesh):
    seq_size, head_count = mesh.devices.shape
    split_mesh = Mesh(mesh.devices.reshape(seq_size // 8, 4, 2, head_count), ("z", "x", "core", "head"))
    seq_axes = ("z", "x", "core")
    placed = (
        P(seq_axes + ("head",), None),
        P(seq_axes + ("head",), None),
        P(seq_axes + ("head",), None),
        P(seq_axes + ("head",), None),
        P(None, "head", seq_axes),
    )
    return jax.shard_map(
        body,
        mesh=split_mesh,
        in_specs=placed,
        out_specs=(P(seq_axes, "head"),) * 4,
        check_vma=False,
    )
```
